256 devices in a mesh: shot: 16 (over y_lo, z), gx: 16 (over y_hi, x, core).
Axes of the slice: x: 4, y: 4 (y_hi: 2, y_lo: 2; y = y_hi * 2 + y_lo), z: 8, core: 2. Of those that a mesh axis runs over, the one named last changes fastest.
Arguments:
- source_prev: float32 [16, 256, 64, 128], P('shot', 'gx'), may hold values from -6 to 6
- source_now: float32 [16, 256, 64, 128], P('shot', 'gx'), may hold values from -6 to 6
- receiver_prev: float32 [16, 256, 64, 128], P('shot', 'gx'), may hold values from -6 to 6
- receiver_now: float32 [16, 256, 64, 128], P('shot', 'gx'), may hold values from -6 to 6
- courant: float32 [256, 64, 128], P('gx'), may hold values from 0.05 to 0.3
- source_cells: int32 [16, 8], P('shot'), may hold values from 0 to 2097151
- wavelet: float32 [16, 2, 8], P('shot'), may hold values from -128 to 128
- receiver_cells: int32 [16, 512], P('shot'), may hold values from 0 to 2097151
- receiver_data: float32 [16, 2, 512], P('shot'), may hold values from -128 to 128
- offsets: int32 [9], replicated, may hold values from -8 to 8, as said below
- conv_weight: float32 [64, 9, 3, 3, 3], replicated, may hold values from -1.25 to 1.25
- conv_bias: float32 [64], replicated, may hold values from -3 to 3
Outputs:
- summary: float32 [64, 64, 512], P(None, 'gx', 'shot')
The draws below stay inside these ranges and needn't reach their ends.
Inputs may be any that keep to these rules, and one draw needn't show every extreme that they name: The offsets are distinct and include -8 and 8.
All inputs are finite; a program needn't handle non-finite values.
Results may differ from the reference program's by a relative error of at most 0.0003.
Values sent between devices are 32-bit elements; how exact they have to be, the bound alone decides.
No kernel may reach another device: no remote copies, remote signals or barrier semaphores. Data moves between devices by JAX's collectives and lax.ppermute only.
A program may use at most 64 MiB of HBM per device.

```python
import jax
import jax.numpy as jnp
from jax import lax

NY = 64
NZ = 128
HMAX = 8
OFFS = 9
OUT_CH = 64
SHOTS = 8
RECS = 512
GROUPS = 16
NX = 256


def draw_offsets(key, part):
    inner = jnp.arange(-HMAX + 1, HMAX, dtype=jnp.int32)
    picked = jax.random.permutation(key, inner)[:OFFS - 2]
    return jnp.concatenate([jnp.array([-HMAX, HMAX], jnp.int32), picked]).astype(jnp.int32)


def set_ends(entries, stream_key, smallest, largest):
    place = [jax.random.randint(jax.random.fold_in(stream_key, axis), (), 0, length) for axis, length in enumerate(entries.shape)]
    widest = entries.shape.index(max(entries.shape))
    beside = place[:widest] + [(place[widest] + 1) % entries.shape[widest]] + place[widest + 1:]
    return entries.at[tuple(place)].set(smallest).at[tuple(beside)].set(largest)


def steps_of(rng, shape, split, least, high):
    def one(dim, parts):
        heights = jax.random.uniform(jax.random.fold_in(jax.random.fold_in(rng, 6), dim), (parts,), jnp.float32, least / len(split), high / len(split))
        return jnp.repeat(jnp.exp(heights), shape[dim] // parts).reshape((-1,) + (1,) * (len(shape) - dim - 1))

    level = one(*split[0])
    for cut in split[1:]:
        level = level * one(*cut)
    return level


def centred(rng, dims, spread, bound, pieces=(), kind=jnp.bfloat16):
    values = jax.random.normal(rng, dims, jnp.float32) * spread
    if len(pieces) > 0:
        values = steps_of(rng, dims, pieces, -0.22, 0.18) * values
    return jnp.clip(values, min=-bound, max=bound).astype(kind)


def setup_inputs(seed: int = 0) -> dict:
    key_of = jax.random.split(jax.random.key(seed), 13)
    return {
        "source_prev": centred(key_of[0], (GROUPS, NX, NY, NZ), 1.0, 6.0, ((0, 16), (1, 16)), jnp.float32),
        "source_now": centred(key_of[1], (GROUPS, NX, NY, NZ), 1.0, 6.0, ((0, 16), (1, 16)), jnp.float32),
        "receiver_prev": centred(key_of[2], (GROUPS, NX, NY, NZ), 1.0, 6.0, ((0, 16), (1, 16)), jnp.float32),
        "receiver_now": centred(key_of[3], (GROUPS, NX, NY, NZ), 1.0, 6.0, ((0, 16), (1, 16)), jnp.float32),
        "courant": jnp.clip(0.05 + 0.25 * jax.random.uniform(key_of[4], (NX, NY, NZ), jnp.float32) ** steps_of(key_of[4], (NX, NY, NZ), ((0, 16),), -0.2, 0.2), 0.05, 0.3),
        "source_cells": set_ends(jax.random.randint(key_of[5], (GROUPS, SHOTS), 0, NX * NY * NZ), jax.random.fold_in(key_of[5], 1), 0, (NX * NY * NZ) - 1).astype(jnp.int32),
        "wavelet": centred(key_of[6], (GROUPS, 2, SHOTS), 20.0, 128.0, ((0, 16),), jnp.float32),
        "receiver_cells": set_ends(jax.random.randint(key_of[7], (GROUPS, RECS), 0, NX * NY * NZ), jax.random.fold_in(key_of[7], 1), 0, (NX * NY * NZ) - 1).astype(jnp.int32),
        "receiver_data": centred(key_of[8], (GROUPS, 2, RECS), 20.0, 128.0, ((0, 16),), jnp.float32),
        "offsets": draw_offsets(jax.random.fold_in(key_of[12], 71), 0),
        "conv_weight": centred(key_of[10], (OUT_CH, OFFS, 3, 3, 3), 27 ** -0.5, 1.25, (), jnp.float32),
        "conv_bias": centred(key_of[11], (OUT_CH,), 0.5, 3.0, (), jnp.float32),
    }


def inject(cells_here, first_x, cell_index, amplitudes, size_y, size_z):
    plane_size = size_y * size_z
    column = cell_index // plane_size
    within = cell_index % plane_size
    local_x = column - first_x
    inside = (local_x >= 0) & (local_x < cells_here)
    target = jnp.where(inside, local_x * plane_size + within, cells_here * plane_size).astype(jnp.int32)
    flat_cells = jnp.zeros((cells_here * plane_size + 1,), jnp.float32).at[target].add(amplitudes.astype(jnp.float32))
    return flat_cells[:-1].reshape(cells_here, size_y, size_z)


def laplace_step(previous, extended, courant, sources):
    center = extended[:, 1:-1]
    padded = jnp.pad(center, ((0, 0), (0, 0), (1, 1), (1, 1)))
    laplace = extended[:, 2:] + extended[:, :-2]
    laplace = laplace + padded[:, :, 2:, 1:-1] + padded[:, :, :-2, 1:-1]
    laplace = laplace + padded[:, :, 1:-1, 2:] + padded[:, :, 1:-1, :-2] - 6.0 * center
    return 2.0 * center - previous + courant * laplace + sources


def coarsen(image_block):
    size_x, size_y, size_z = image_block.shape
    return image_block.reshape(size_x // 4, 4, size_y // 4, 4, size_z // 4, 4).mean(axis=(1, 3, 5))


def offset_image(wide, offsets, margin, cells_x):
    def per_offset(offset_value):
        forward_part = lax.dynamic_slice_in_dim(wide, (margin + offset_value).astype(jnp.int32), cells_x, 1)
        backward_part = lax.dynamic_slice_in_dim(wide, (margin - offset_value).astype(jnp.int32), cells_x, 1)
        image_block = forward_part[0] * backward_part[1] + forward_part[2] * backward_part[3]
        return coarsen(image_block)
    return lax.map(per_offset, offsets)


def conv_apply(padded, conv_weight, conv_bias):
    channels, span_x, span_y, span_z = padded.shape
    size_x, size_y, size_z = span_x - 2, span_y - 2, span_z - 2
    patches = jnp.stack([padded[:, step_x:step_x + size_x, step_y:step_y + size_y, step_z:step_z + size_z]
                         for step_x in range(3) for step_y in range(3) for step_z in range(3)], axis=1)
    patches = patches.reshape(channels * 27, size_x * size_y * size_z)
    matrix = conv_weight.reshape(conv_weight.shape[0], channels * 27)
    result = jnp.dot(matrix, patches, precision=lax.Precision.HIGHEST, preferred_element_type=jnp.float32)
    result = result + conv_bias[:, None]
    return result.reshape(conv_weight.shape[0], size_x, size_y * size_z)


def reference(source_prev, source_now, receiver_prev, receiver_now, courant, source_cells, wavelet, receiver_cells, receiver_data, offsets, conv_weight, conv_bias):
    grid_x, size_y, size_z = courant.shape

    def per_group(packed):
        s_prev, s_now, r_prev, r_now, s_cells, s_amp, r_cells, r_amp = packed
        previous = jnp.stack([s_prev, r_prev])
        current = jnp.stack([s_now, r_now])
        levels = []
        for step_index in range(2):
            extended = jnp.pad(current, ((0, 0), (1, 1), (0, 0), (0, 0)))
            sources = jnp.stack([inject(grid_x, 0, s_cells, s_amp[step_index], size_y, size_z),
                                 inject(grid_x, 0, r_cells, r_amp[step_index], size_y, size_z)])
            advanced = laplace_step(previous, extended, courant, sources)
            previous, current = current, advanced
            levels.append(advanced)
        fields = jnp.concatenate(levels, axis=0)
        wide = jnp.pad(fields, ((0, 0), (HMAX, HMAX), (0, 0), (0, 0)))
        return offset_image(wide, offsets, HMAX, grid_x)

    coarse = lax.map(per_group, (source_prev, source_now, receiver_prev, receiver_now,
                                 source_cells, wavelet, receiver_cells, receiver_data))
    summed = jnp.sum(coarse, axis=0)
    padded = jnp.pad(summed, ((0, 0), (1, 1), (1, 1), (1, 1)))
    return conv_apply(padded, conv_weight, conv_bias)
```

```python
import jax
import jax.numpy as jnp
from jax import lax
from jax.sharding import PartitionSpec as P

HMAX = 8


def padded_2(block, sides, width):
    for axis, dim in sides:
        count = lax.axis_size(axis)
        forward = [(i, i + 1) for i in range(count - 1)]
        backward = [(target, source) for source, target in forward]
        low = lax.ppermute(
            lax.slice_in_dim(block, block.shape[dim] - width, None, axis=dim), axis, forward
        )
        high = lax.ppermute(lax.slice_in_dim(block, 0, width, axis=dim), axis, backward)
        block = jnp.concatenate([low, block, high], axis=dim)
    return block


def inject(cells_here, first_x, cell_index, amplitudes, size_y, size_z):
    plane_size = size_y * size_z
    column = cell_index // plane_size
    within = cell_index % plane_size
    local_x = column - first_x
    inside = (local_x >= 0) & (local_x < cells_here)
    target = jnp.where(inside, local_x * plane_size + within, cells_here * plane_size)
    flat_cells = jnp.zeros((cells_here * plane_size + 1,), jnp.float32).at[target].add(amplitudes)
    return flat_cells[:-1].reshape(cells_here, size_y, size_z)


def laplace_step(previous, extended, courant, sources):
    center = extended[:, 1:-1]
    padded = jnp.pad(center, ((0, 0), (0, 0), (1, 1), (1, 1)))
    laplace = extended[:, 2:] + extended[:, :-2]
    laplace = laplace + padded[:, :, 2:, 1:-1] + padded[:, :, :-2, 1:-1]
    laplace = laplace + padded[:, :, 1:-1, 2:] + padded[:, :, 1:-1, :-2] - 6.0 * center
    return 2.0 * center - previous + courant * laplace + sources


def pooling(size, group):
    fine = jnp.arange(size)[:, None] // group
    coarse = jnp.arange(size // group)[None, :]
    return (fine == coarse).astype(jnp.float32)


def offset_image(wide, offsets, margin, cells_x):
    _, _, size_y, size_z = wide.shape
    parts = []
    for index in range(offsets.shape[0]):
        offset_value = offsets[index]
        forward_part = lax.dynamic_slice_in_dim(wide, margin + offset_value, cells_x, 1)
        backward_part = lax.dynamic_slice_in_dim(wide, margin - offset_value, cells_x, 1)
        image_block = forward_part[0] * backward_part[1] + forward_part[2] * backward_part[3]
        parts.append(image_block.reshape(cells_x // 4, 4, size_y, size_z).sum(axis=1))
    pooled_x = jnp.stack(parts)
    pooled_z = jnp.einsum(
        "ixyz,zc->ixyc", pooled_x, pooling(size_z, 4), precision=lax.Precision.HIGHEST
    )
    pooled = jnp.einsum(
        "yb,ixyc->ixbc", pooling(size_y, 4), pooled_z, precision=lax.Precision.HIGHEST
    )
    return pooled * (1.0 / 64.0)


def conv_apply(padded, conv_weight, conv_bias):
    channels, span_x, span_y, span_z = padded.shape
    size_x, size_y, size_z = (span_x - 2, span_y - 2, span_z - 2)
    patches = jnp.stack(
        [
            padded[:, step_x : step_x + size_x, step_y : step_y + size_y, step_z : step_z + size_z]
            for step_x in range(3)
            for step_y in range(3)
            for step_z in range(3)
        ],
        axis=1,
    )
    patches = patches.reshape(channels * 27, size_x * size_y * size_z)
    matrix = conv_weight.reshape(conv_weight.shape[0], channels * 27)
    result = jnp.dot(
        matrix, patches, precision=lax.Precision.HIGHEST, preferred_element_type=jnp.float32
    )
    result = result + conv_bias[:, None]
    return result.reshape(conv_weight.shape[0], size_x, size_y * size_z)


def group_sum_windows(coarse, axis):
    count = lax.axis_size(axis)
    rows = coarse.shape[2] // count
    rimmed = jnp.pad(coarse, ((0, 0), (0, 0), (1, 1), (0, 0)))
    windows = jnp.stack(
        [lax.slice_in_dim(rimmed, member * rows, member * rows + rows + 2, axis=2) for member in range(count)]
    )
    received = lax.all_to_all(windows, axis, 0, 0, tiled=True)
    return received.sum(axis=0)


def local(
    source_prev,
    source_now,
    receiver_prev,
    receiver_now,
    courant,
    source_cells,
    wavelet,
    receiver_cells,
    receiver_data,
    offsets,
    conv_weight,
    conv_bias,
):
    cells_x, size_y, size_z = courant.shape
    slab_index = lax.axis_index("gx")
    previous = jnp.stack([source_prev[0], receiver_prev[0]])
    current = jnp.stack([source_now[0], receiver_now[0]])
    levels = []
    for step_index in range(2):
        extended = padded_2(current, (("gx", 1),), 1)
        first_x = slab_index * cells_x
        advanced = laplace_step(
            previous,
            extended,
            courant,
            jnp.stack(
                [
                    inject(
                        cells_x, first_x, source_cells[0], wavelet[0, step_index], size_y, size_z
                    ),
                    inject(
                        cells_x,
                        first_x,
                        receiver_cells[0],
                        receiver_data[0, step_index],
                        size_y,
                        size_z,
                    ),
                ]
            ),
        )
        previous, current = (current, advanced)
        levels.append(advanced)
    fields = jnp.concatenate(levels, axis=0)
    wide = padded_2(fields, (("gx", 1),), HMAX)
    coarse = offset_image(wide, offsets, HMAX, cells_x)
    summed = group_sum_windows(coarse, "shot")
    rimmed = padded_2(summed, (("gx", 1),), 1)
    window = jnp.pad(rimmed, ((0, 0), (0, 0), (0, 0), (1, 1)))
    return conv_apply(window, conv_weight, conv_bias)


def solution(mesh):
    in_specs = (
        P("shot", "gx", None, None),
        P("shot", "gx", None, None),
        P("shot", "gx", None, None),
        P("shot", "gx", None, None),
        P("gx", None, None),
        P("shot", None),
        P("shot", None, None),
        P("shot", None),
        P("shot", None, None),
        P(),
        P(),
        P(),
    )
    out_specs = P(None, "gx", "shot")
    return jax.shard_map(local, mesh=mesh, in_specs=in_specs, out_specs=out_specs, check_vma=False)
```

```python
import jax
import jax.numpy as jnp
from jax import lax
from jax.sharding import PartitionSpec as P

HMAX = 8


def padded_2(block, sides, width):
    for axis, dim in sides:
        count = lax.axis_size(axis)
        forward = [(i, i + 1) for i in range(count - 1)]
        backward = [(target, source) for source, target in forward]
        low = lax.ppermute(
            lax.slice_in_dim(block, block.shape[dim] - width, None, axis=dim), axis, forward
        )
        high = lax.ppermute(lax.slice_in_dim(block, 0, width, axis=dim), axis, backward)
        block = jnp.concatenate([low, block, high], axis=dim)
    return block


def input_halo(current, previous, courant, axis):
    count = lax.axis_size(axis)
    forward = [(i, i + 1) for i in range(count - 1)]
    backward = [(target, source) for source, target in forward]
    fields, cells_x, size_y, size_z = current.shape

    def pack(now_planes, prev_planes, courant_planes):
        return jnp.concatenate(
            [now_planes.reshape(-1, size_y, size_z), prev_planes.reshape(-1, size_y, size_z), courant_planes]
        )

    def unpack(planes):
        now_planes = planes[: 2 * fields].reshape(fields, 2, size_y, size_z)
        prev_planes = planes[2 * fields : 3 * fields].reshape(fields, 1, size_y, size_z)
        return now_planes, prev_planes, planes[3 * fields :]

    low = lax.ppermute(
        pack(current[:, -2:], previous[:, -1:], courant[-1:]), axis, forward
    )
    high = lax.ppermute(pack(current[:, :2], previous[:, :1], courant[:1]), axis, backward)
    low_now, low_prev, low_courant = unpack(low)
    high_now, high_prev, high_courant = unpack(high)
    current_wide = jnp.concatenate([low_now, current, high_now], axis=1)
    previous_wide = jnp.concatenate([low_prev, previous, high_prev], axis=1)
    courant_wide = jnp.concatenate([low_courant, courant, high_courant], axis=0)
    return current_wide, previous_wide, courant_wide


def inject(cells_here, first_x, cell_index, amplitudes, size_y, size_z):
    plane_size = size_y * size_z
    column = cell_index // plane_size
    within = cell_index % plane_size
    local_x = column - first_x
    inside = (local_x >= 0) & (local_x < cells_here)
    target = jnp.where(inside, local_x * plane_size + within, cells_here * plane_size)
    flat_cells = jnp.zeros((cells_here * plane_size + 1,), jnp.float32).at[target].add(amplitudes)
    return flat_cells[:-1].reshape(cells_here, size_y, size_z)


def laplace_step(previous, extended, courant, sources):
    center = extended[:, 1:-1]
    padded = jnp.pad(center, ((0, 0), (0, 0), (1, 1), (1, 1)))
    laplace = extended[:, 2:] + extended[:, :-2]
    laplace = laplace + padded[:, :, 2:, 1:-1] + padded[:, :, :-2, 1:-1]
    laplace = laplace + padded[:, :, 1:-1, 2:] + padded[:, :, 1:-1, :-2] - 6.0 * center
    return 2.0 * center - previous + courant * laplace + sources


def pooling(size, group):
    fine = jnp.arange(size)[:, None] // group
    coarse = jnp.arange(size // group)[None, :]
    return (fine == coarse).astype(jnp.float32)


def offset_image(wide, offsets, margin, cells_x):
    _, _, size_y, size_z = wide.shape
    parts = []
    for index in range(offsets.shape[0]):
        offset_value = offsets[index]
        forward_part = lax.dynamic_slice_in_dim(wide, margin + offset_value, cells_x, 1)
        backward_part = lax.dynamic_slice_in_dim(wide, margin - offset_value, cells_x, 1)
        image_block = forward_part[0] * backward_part[1] + forward_part[2] * backward_part[3]
        parts.append(image_block.reshape(cells_x // 4, 4, size_y, size_z).sum(axis=1))
    pooled_x = jnp.stack(parts)
    pooled_z = jnp.einsum(
        "ixyz,zc->ixyc", pooled_x, pooling(size_z, 4), precision=lax.Precision.HIGHEST
    )
    pooled = jnp.einsum(
        "yb,ixyc->ixbc", pooling(size_y, 4), pooled_z, precision=lax.Precision.HIGHEST
    )
    return pooled * (1.0 / 64.0)


def conv_apply(padded, conv_weight, conv_bias):
    channels, span_x, span_y, span_z = padded.shape
    size_x, size_y, size_z = (span_x - 2, span_y - 2, span_z - 2)
    patches = jnp.stack(
        [
            padded[:, step_x : step_x + size_x, step_y : step_y + size_y, step_z : step_z + size_z]
            for step_x in range(3)
            for step_y in range(3)
            for step_z in range(3)
        ],
        axis=1,
    )
    patches = patches.reshape(channels * 27, size_x * size_y * size_z)
    matrix = conv_weight.reshape(conv_weight.shape[0], channels * 27)
    result = jnp.dot(
        matrix, patches, precision=lax.Precision.HIGHEST, preferred_element_type=jnp.float32
    )
    result = result + conv_bias[:, None]
    return result.reshape(conv_weight.shape[0], size_x, size_y * size_z)


def group_sum_windows(coarse, axis):
    count = lax.axis_size(axis)
    rows = coarse.shape[2] // count
    rimmed = jnp.pad(coarse, ((0, 0), (0, 0), (1, 1), (0, 0)))
    windows = jnp.stack(
        [lax.slice_in_dim(rimmed, member * rows, member * rows + rows + 2, axis=2) for member in range(count)]
    )
    received = lax.all_to_all(windows, axis, 0, 0, tiled=True)
    return received.sum(axis=0)


def local(
    source_prev,
    source_now,
    receiver_prev,
    receiver_now,
    courant,
    source_cells,
    wavelet,
    receiver_cells,
    receiver_data,
    offsets,
    conv_weight,
    conv_bias,
):
    cells_x, size_y, size_z = courant.shape
    slab_index = lax.axis_index("gx")
    first_x = slab_index * cells_x
    previous = jnp.stack([source_prev[0], receiver_prev[0]])
    current = jnp.stack([source_now[0], receiver_now[0]])
    current_wide, previous_wide, courant_wide = input_halo(current, previous, courant, "gx")
    levels = []
    for step_index in range(2):
        if step_index == 0:
            cells_here, first_here = cells_x + 2, first_x - 1
            step_previous, step_extended, step_courant = previous_wide, current_wide, courant_wide
        else:
            cells_here, first_here = cells_x, first_x
            step_previous, step_extended, step_courant = current, levels[0], courant
        sources = jnp.stack(
            [
                inject(cells_here, first_here, source_cells[0], wavelet[0, step_index], size_y, size_z),
                inject(
                    cells_here, first_here, receiver_cells[0], receiver_data[0, step_index], size_y, size_z
                ),
            ]
        )
        advanced = laplace_step(step_previous, step_extended, step_courant, sources)
        levels.append(advanced)
    levels[0] = levels[0][:, 1:-1]
    fields = jnp.concatenate(levels, axis=0)
    wide = padded_2(fields, (("gx", 1),), HMAX)
    coarse = offset_image(wide, offsets, HMAX, cells_x)
    summed = group_sum_windows(coarse, "shot")
    rimmed = padded_2(summed, (("gx", 1),), 1)
    window = jnp.pad(rimmed, ((0, 0), (0, 0), (0, 0), (1, 1)))
    return conv_apply(window, conv_weight, conv_bias)


def solution(mesh):
    in_specs = (
        P("shot", "gx", None, None),
        P("shot", "gx", None, None),
        P("shot", "gx", None, None),
        P("shot", "gx", None, None),
        P("gx", None, None),
        P("shot", None),
        P("shot", None, None),
        P("shot", None),
        P("shot", None, None),
        P(),
        P(),
        P(),
    )
    out_specs = P(None, "gx", "shot")
    return jax.shard_map(local, mesh=mesh, in_specs=in_specs, out_specs=out_specs, check_vma=False)
```

```python
import jax
import jax.numpy as jnp
from jax import lax
from jax.sharding import PartitionSpec as P

HMAX = 8


def padded_2(block, sides, width):
    for axis, dim in sides:
        count = lax.axis_size(axis)
        forward = [(i, i + 1) for i in range(count - 1)]
        backward = [(target, source) for source, target in forward]
        low = lax.ppermute(
            lax.slice_in_dim(block, block.shape[dim] - width, None, axis=dim), axis, forward
        )
        high = lax.ppermute(lax.slice_in_dim(block, 0, width, axis=dim), axis, backward)
        block = jnp.concatenate([low, block, high], axis=dim)
    return block


def input_halo(arrays, width, axis):
    count = lax.axis_size(axis)
    forward = [(i, i + 1) for i in range(count - 1)]
    backward = [(target, source) for source, target in forward]
    low = lax.ppermute(jnp.concatenate([array[-width:] for array in arrays]), axis, forward)
    high = lax.ppermute(jnp.concatenate([array[:width] for array in arrays]), axis, backward)
    return [
        jnp.concatenate([low[k * width : (k + 1) * width], array, high[k * width : (k + 1) * width]])
        for k, array in enumerate(arrays)
    ]


def inject(cells_here, first_x, cell_index, amplitudes, size_y, size_z):
    plane_size = size_y * size_z
    column = cell_index // plane_size
    within = cell_index % plane_size
    local_x = column - first_x
    inside = (local_x >= 0) & (local_x < cells_here)
    target = jnp.where(inside, local_x * plane_size + within, cells_here * plane_size)
    flat_cells = jnp.zeros((cells_here * plane_size + 1,), jnp.float32).at[target].add(amplitudes)
    return flat_cells[:-1].reshape(cells_here, size_y, size_z)


def laplace_step(previous, extended, courant, sources):
    center = extended[:, 1:-1]
    padded = jnp.pad(center, ((0, 0), (0, 0), (1, 1), (1, 1)))
    laplace = extended[:, 2:] + extended[:, :-2]
    laplace = laplace + padded[:, :, 2:, 1:-1] + padded[:, :, :-2, 1:-1]
    laplace = laplace + padded[:, :, 1:-1, 2:] + padded[:, :, 1:-1, :-2] - 6.0 * center
    return 2.0 * center - previous + courant * laplace + sources


def pooling(size, group):
    fine = jnp.arange(size)[:, None] // group
    coarse = jnp.arange(size // group)[None, :]
    return (fine == coarse).astype(jnp.float32)


def offset_image(wide, offsets, margin, cells_x):
    _, _, size_y, size_z = wide.shape
    parts = []
    for index in range(offsets.shape[0]):
        offset_value = offsets[index]
        forward_part = lax.dynamic_slice_in_dim(wide, margin + offset_value, cells_x, 1)
        backward_part = lax.dynamic_slice_in_dim(wide, margin - offset_value, cells_x, 1)
        image_block = forward_part[0] * backward_part[1] + forward_part[2] * backward_part[3]
        parts.append(image_block.reshape(cells_x // 4, 4, size_y, size_z).sum(axis=1))
    pooled_x = jnp.stack(parts)
    pooled_z = jnp.einsum(
        "ixyz,zc->ixyc", pooled_x, pooling(size_z, 4), precision=lax.Precision.HIGHEST
    )
    pooled = jnp.einsum(
        "yb,ixyc->ixbc", pooling(size_y, 4), pooled_z, precision=lax.Precision.HIGHEST
    )
    return pooled * (1.0 / 64.0)


def conv_apply(padded, conv_weight, conv_bias):
    channels, span_x, span_y, span_z = padded.shape
    size_x, size_y, size_z = (span_x - 2, span_y - 2, span_z - 2)
    patches = jnp.stack(
        [
            padded[:, step_x : step_x + size_x, step_y : step_y + size_y, step_z : step_z + size_z]
            for step_x in range(3)
            for step_y in range(3)
            for step_z in range(3)
        ],
        axis=1,
    )
    patches = patches.reshape(channels * 27, size_x * size_y * size_z)
    matrix = conv_weight.reshape(conv_weight.shape[0], channels * 27)
    result = jnp.dot(
        matrix, patches, precision=lax.Precision.HIGHEST, preferred_element_type=jnp.float32
    )
    result = result + conv_bias[:, None]
    return result.reshape(conv_weight.shape[0], size_x, size_y * size_z)


def group_sum_windows(coarse, axis):
    count = lax.axis_size(axis)
    rows = coarse.shape[2] // count
    rimmed = jnp.pad(coarse, ((0, 0), (0, 0), (1, 1), (0, 0)))
    windows = jnp.stack(
        [lax.slice_in_dim(rimmed, member * rows, member * rows + rows + 2, axis=2) for member in range(count)]
    )
    received = lax.all_to_all(windows, axis, 0, 0, tiled=True)
    return received.sum(axis=0)


def local(
    source_prev,
    source_now,
    receiver_prev,
    receiver_now,
    courant,
    source_cells,
    wavelet,
    receiver_cells,
    receiver_data,
    offsets,
    conv_weight,
    conv_bias,
):
    cells_x, size_y, size_z = courant.shape
    margin = HMAX + 2
    assert margin <= cells_x
    first_x = lax.axis_index("gx") * cells_x
    source_prev_w, source_now_w, receiver_prev_w, receiver_now_w, courant_w = input_halo(
        [source_prev[0], source_now[0], receiver_prev[0], receiver_now[0], courant], margin, "gx"
    )
    previous = jnp.stack([source_prev_w, receiver_prev_w])
    current = jnp.stack([source_now_w, receiver_now_w])
    levels = []
    for step_index in range(2):
        trim = step_index + 1
        cells_here = cells_x + 2 * (margin - trim)
        sources = jnp.stack(
            [
                inject(cells_here, first_x - margin + trim, source_cells[0], wavelet[0, step_index], size_y, size_z),
                inject(
                    cells_here,
                    first_x - margin + trim,
                    receiver_cells[0],
                    receiver_data[0, step_index],
                    size_y,
                    size_z,
                ),
            ]
        )
        advanced = laplace_step(
            previous[:, trim : trim + cells_here],
            current,
            courant_w[trim : trim + cells_here],
            sources,
        )
        previous, current = (current, advanced)
        levels.append(advanced)
    wide = jnp.concatenate([levels[0][:, 1:-1], levels[1]], axis=0)
    coarse = offset_image(wide, offsets, HMAX, cells_x)
    summed = group_sum_windows(coarse, "shot")
    rimmed = padded_2(summed, (("gx", 1),), 1)
    window = jnp.pad(rimmed, ((0, 0), (0, 0), (0, 0), (1, 1)))
    return conv_apply(window, conv_weight, conv_bias)


def solution(mesh):
    in_specs = (
        P("shot", "gx", None, None),
        P("shot", "gx", None, None),
        P("shot", "gx", None, None),
        P("shot", "gx", None, None),
        P("gx", None, None),
        P("shot", None),
        P("shot", None, None),
        P("shot", None),
        P("shot", None, None),
        P(),
        P(),
        P(),
    )
    out_specs = P(None, "gx", "shot")
    return jax.shard_map(local, mesh=mesh, in_specs=in_specs, out_specs=out_specs, check_vma=False)
```

```python
import jax
import jax.numpy as jnp
from jax import lax
from jax.experimental import pallas as pl
from jax.experimental.pallas import tpu as pltpu
from jax.sharding import PartitionSpec as P

HMAX = 8


def padded_2(block, sides, width):
    for axis, dim in sides:
        count = lax.axis_size(axis)
        forward = [(i, i + 1) for i in range(count - 1)]
        backward = [(target, source) for source, target in forward]
        low = lax.ppermute(
            lax.slice_in_dim(block, block.shape[dim] - width, None, axis=dim), axis, forward
        )
        high = lax.ppermute(lax.slice_in_dim(block, 0, width, axis=dim), axis, backward)
        block = jnp.concatenate([low, block, high], axis=dim)
    return block


def input_halo(current, previous, courant, axis):
    count = lax.axis_size(axis)
    forward = [(i, i + 1) for i in range(count - 1)]
    backward = [(target, source) for source, target in forward]
    fields, cells_x, size_y, size_z = current.shape

    def pack(now_planes, prev_planes, courant_planes):
        return jnp.concatenate(
            [now_planes.reshape(-1, size_y, size_z), prev_planes.reshape(-1, size_y, size_z), courant_planes]
        )

    def unpack(planes):
        now_planes = planes[: 2 * fields].reshape(fields, 2, size_y, size_z)
        prev_planes = planes[2 * fields : 3 * fields].reshape(fields, 1, size_y, size_z)
        return now_planes, prev_planes, planes[3 * fields :]

    low = lax.ppermute(
        pack(current[:, -2:], previous[:, -1:], courant[-1:]), axis, forward
    )
    high = lax.ppermute(pack(current[:, :2], previous[:, :1], courant[:1]), axis, backward)
    low_now, low_prev, low_courant = unpack(low)
    high_now, high_prev, high_courant = unpack(high)
    current_wide = jnp.concatenate([low_now, current, high_now], axis=1)
    previous_wide = jnp.concatenate([low_prev, previous, high_prev], axis=1)
    courant_wide = jnp.concatenate([low_courant, courant, high_courant], axis=0)
    return current_wide, previous_wide, courant_wide


def inject(cells_here, first_x, cell_index, amplitudes, size_y, size_z):
    plane_size = size_y * size_z
    column = cell_index // plane_size
    within = cell_index % plane_size
    local_x = column - first_x
    inside = (local_x >= 0) & (local_x < cells_here)
    target = jnp.where(inside, local_x * plane_size + within, cells_here * plane_size)
    flat_cells = jnp.zeros((cells_here * plane_size + 1,), jnp.float32).at[target].add(amplitudes)
    return flat_cells[:-1].reshape(cells_here, size_y, size_z)


def laplace_step(previous, extended, courant, sources):
    center = extended[:, 1:-1]
    padded = jnp.pad(center, ((0, 0), (0, 0), (1, 1), (1, 1)))
    laplace = extended[:, 2:] + extended[:, :-2]
    laplace = laplace + padded[:, :, 2:, 1:-1] + padded[:, :, :-2, 1:-1]
    laplace = laplace + padded[:, :, 1:-1, 2:] + padded[:, :, 1:-1, :-2] - 6.0 * center
    return 2.0 * center - previous + courant * laplace + sources


def pooling(size, group):
    fine = jnp.arange(size)[:, None] // group
    coarse = jnp.arange(size // group)[None, :]
    return (fine == coarse).astype(jnp.float32)


def split_dot(left, right, split_left):
    def parts(value):
        high = value.astype(jnp.bfloat16)
        rest = value - high.astype(jnp.float32)
        middle = rest.astype(jnp.bfloat16)
        low = (rest - middle.astype(jnp.float32)).astype(jnp.bfloat16)
        return (high, middle, low)

    total = None
    if split_left:
        pieces = [(piece, right.astype(jnp.bfloat16)) for piece in parts(left)]
    else:
        pieces = [(left.astype(jnp.bfloat16), piece) for piece in parts(right)]
    for a, b in pieces:
        term = jnp.dot(a, b, preferred_element_type=jnp.float32)
        total = term if total is None else total + term
    return total


def offset_image(wide, offsets, margin, cells_x):
    fields, span_x, size_y, size_z = wide.shape
    count = offsets.shape[0]
    blocks_x, blocks_y, blocks_z = cells_x // 4, size_y // 4, size_z // 4
    pool_z = pooling(size_z, 4)
    pool_y = (
        (jnp.arange(blocks_x * size_y)[None, :] // 4) == jnp.arange(blocks_x * blocks_y)[:, None]
    ).astype(jnp.float32)

    def kernel(offsets_ref, wide_ref, pool_z_ref, pool_y_ref, out_ref):
        offset_value = offsets_ref[pl.program_id(0)]
        forward = margin + offset_value
        backward = margin - offset_value
        rows = []
        for block in range(blocks_x):
            total = None
            for step in range(4):
                x = block * 4 + step
                term = (
                    wide_ref[0, forward + x] * wide_ref[1, backward + x]
                    + wide_ref[2, forward + x] * wide_ref[3, backward + x]
                )
                total = term if total is None else total + term
            rows.append(total)
        pooled_x = jnp.concatenate(rows, axis=0)
        pooled_z = split_dot(pooled_x, pool_z_ref[...], True)
        pooled = split_dot(pool_y_ref[...], pooled_z, False)
        out_ref[0] = (pooled * (1.0 / 64.0)).reshape(blocks_x, blocks_y, blocks_z)

    return pl.pallas_call(
        kernel,
        grid_spec=pltpu.PrefetchScalarGridSpec(
            num_scalar_prefetch=1,
            grid=(count,),
            in_specs=[
                pl.BlockSpec((fields, span_x, size_y, size_z), lambda i, offsets_ref: (0, 0, 0, 0)),
                pl.BlockSpec((size_z, blocks_z), lambda i, offsets_ref: (0, 0)),
                pl.BlockSpec((blocks_x * blocks_y, blocks_x * size_y), lambda i, offsets_ref: (0, 0)),
            ],
            out_specs=pl.BlockSpec((1, blocks_x, blocks_y, blocks_z), lambda i, offsets_ref: (i, 0, 0, 0)),
        ),
        out_shape=jax.ShapeDtypeStruct((count, blocks_x, blocks_y, blocks_z), jnp.float32),
    )(offsets, wide, pool_z, pool_y)


def conv_apply(padded, conv_weight, conv_bias):
    channels, span_x, span_y, span_z = padded.shape
    size_x, size_y, size_z = (span_x - 2, span_y - 2, span_z - 2)
    patches = jnp.stack(
        [
            padded[:, step_x : step_x + size_x, step_y : step_y + size_y, step_z : step_z + size_z]
            for step_x in range(3)
            for step_y in range(3)
            for step_z in range(3)
        ],
        axis=1,
    )
    patches = patches.reshape(channels * 27, size_x * size_y * size_z)
    matrix = conv_weight.reshape(conv_weight.shape[0], channels * 27)
    result = jnp.dot(
        matrix, patches, precision=lax.Precision.HIGHEST, preferred_element_type=jnp.float32
    )
    result = result + conv_bias[:, None]
    return result.reshape(conv_weight.shape[0], size_x, size_y * size_z)


def group_sum_windows(coarse, axis):
    count = lax.axis_size(axis)
    rows = coarse.shape[2] // count
    rimmed = jnp.pad(coarse, ((0, 0), (0, 0), (1, 1), (0, 0)))
    windows = jnp.stack(
        [lax.slice_in_dim(rimmed, member * rows, member * rows + rows + 2, axis=2) for member in range(count)]
    )
    received = lax.all_to_all(windows, axis, 0, 0, tiled=True)
    return received.sum(axis=0)


def local(
    source_prev,
    source_now,
    receiver_prev,
    receiver_now,
    courant,
    source_cells,
    wavelet,
    receiver_cells,
    receiver_data,
    offsets,
    conv_weight,
    conv_bias,
):
    cells_x, size_y, size_z = courant.shape
    slab_index = lax.axis_index("gx")
    first_x = slab_index * cells_x
    previous = jnp.stack([source_prev[0], receiver_prev[0]])
    current = jnp.stack([source_now[0], receiver_now[0]])
    current_wide, previous_wide, courant_wide = input_halo(current, previous, courant, "gx")
    levels = []
    for step_index in range(2):
        if step_index == 0:
            cells_here, first_here = cells_x + 2, first_x - 1
            step_previous, step_extended, step_courant = previous_wide, current_wide, courant_wide
        else:
            cells_here, first_here = cells_x, first_x
            step_previous, step_extended, step_courant = current, levels[0], courant
        sources = jnp.stack(
            [
                inject(cells_here, first_here, source_cells[0], wavelet[0, step_index], size_y, size_z),
                inject(
                    cells_here, first_here, receiver_cells[0], receiver_data[0, step_index], size_y, size_z
                ),
            ]
        )
        advanced = laplace_step(step_previous, step_extended, step_courant, sources)
        levels.append(advanced)
    levels[0] = levels[0][:, 1:-1]
    fields = jnp.concatenate(levels, axis=0)
    wide = padded_2(fields, (("gx", 1),), HMAX)
    coarse = offset_image(wide, offsets, HMAX, cells_x)
    summed = group_sum_windows(coarse, "shot")
    rimmed = padded_2(summed, (("gx", 1),), 1)
    window = jnp.pad(rimmed, ((0, 0), (0, 0), (0, 0), (1, 1)))
    return conv_apply(window, conv_weight, conv_bias)


def solution(mesh):
    in_specs = (
        P("shot", "gx", None, None),
        P("shot", "gx", None, None),
        P("shot", "gx", None, None),
        P("shot", "gx", None, None),
        P("gx", None, None),
        P("shot", None),
        P("shot", None, None),
        P("shot", None),
        P("shot", None, None),
        P(),
        P(),
        P(),
    )
    out_specs = P(None, "gx", "shot")
    return jax.shard_map(local, mesh=mesh, in_specs=in_specs, out_specs=out_specs, check_vma=False)
```

```python
import jax
import jax.numpy as jnp
from jax import lax
from jax.experimental import pallas as pl
from jax.experimental.pallas import tpu as pltpu
from jax.sharding import PartitionSpec as P

HMAX = 8


def padded_2(block, sides, width):
    for axis, dim in sides:
        count = lax.axis_size(axis)
        forward = [(i, i + 1) for i in range(count - 1)]
        backward = [(target, source) for source, target in forward]
        low = lax.ppermute(
            lax.slice_in_dim(block, block.shape[dim] - width, None, axis=dim), axis, forward
        )
        high = lax.ppermute(lax.slice_in_dim(block, 0, width, axis=dim), axis, backward)
        block = jnp.concatenate([low, block, high], axis=dim)
    return block


def input_halo(current, previous, courant, axis):
    count = lax.axis_size(axis)
    forward = [(i, i + 1) for i in range(count - 1)]
    backward = [(target, source) for source, target in forward]
    fields, cells_x, size_y, size_z = current.shape

    def pack(now_planes, prev_planes, courant_planes):
        return jnp.concatenate(
            [now_planes.reshape(-1, size_y, size_z), prev_planes.reshape(-1, size_y, size_z), courant_planes]
        )

    def unpack(planes):
        now_planes = planes[: 2 * fields].reshape(fields, 2, size_y, size_z)
        prev_planes = planes[2 * fields : 3 * fields].reshape(fields, 1, size_y, size_z)
        return now_planes, prev_planes, planes[3 * fields :]

    low = lax.ppermute(
        pack(current[:, -2:], previous[:, -1:], courant[-1:]), axis, forward
    )
    high = lax.ppermute(pack(current[:, :2], previous[:, :1], courant[:1]), axis, backward)
    low_now, low_prev, low_courant = unpack(low)
    high_now, high_prev, high_courant = unpack(high)
    current_wide = jnp.concatenate([low_now, current, high_now], axis=1)
    previous_wide = jnp.concatenate([low_prev, previous, high_prev], axis=1)
    courant_wide = jnp.concatenate([low_courant, courant, high_courant], axis=0)
    return current_wide, previous_wide, courant_wide


def inject(cells_here, first_x, cell_index, amplitudes, size_y, size_z):
    plane_size = size_y * size_z
    column = cell_index // plane_size
    within = cell_index % plane_size
    local_x = column - first_x
    inside = (local_x >= 0) & (local_x < cells_here)
    target = jnp.where(inside, local_x * plane_size + within, cells_here * plane_size)
    flat_cells = jnp.zeros((cells_here * plane_size + 1,), jnp.float32).at[target].add(amplitudes)
    return flat_cells[:-1].reshape(cells_here, size_y, size_z)


def laplace_step(previous, extended, courant, sources):
    center = extended[:, 1:-1]
    padded = jnp.pad(center, ((0, 0), (0, 0), (1, 1), (1, 1)))
    laplace = extended[:, 2:] + extended[:, :-2]
    laplace = laplace + padded[:, :, 2:, 1:-1] + padded[:, :, :-2, 1:-1]
    laplace = laplace + padded[:, :, 1:-1, 2:] + padded[:, :, 1:-1, :-2] - 6.0 * center
    return 2.0 * center - previous + courant * laplace + sources


def pooling(size, group):
    fine = jnp.arange(size)[:, None] // group
    coarse = jnp.arange(size // group)[None, :]
    return (fine == coarse).astype(jnp.float32)


def split_dot(left, right, split_left):
    def parts(value):
        high = value.astype(jnp.bfloat16)
        rest = value - high.astype(jnp.float32)
        middle = rest.astype(jnp.bfloat16)
        low = (rest - middle.astype(jnp.float32)).astype(jnp.bfloat16)
        return (high, middle, low)

    total = None
    if split_left:
        pieces = [(piece, right.astype(jnp.bfloat16)) for piece in parts(left)]
    else:
        pieces = [(left.astype(jnp.bfloat16), piece) for piece in parts(right)]
    for a, b in pieces:
        term = jnp.dot(a, b, preferred_element_type=jnp.float32)
        total = term if total is None else total + term
    return total


def offset_image(wide, offsets, margin, cells_x):
    fields, span_x, size_y, size_z = wide.shape
    count = offsets.shape[0]
    blocks_x, blocks_y, blocks_z = cells_x // 4, size_y // 4, size_z // 4
    pool_z = pooling(size_z, 4)
    pool_y = (
        (jnp.arange(blocks_x * size_y)[None, :] // 4) == jnp.arange(blocks_x * blocks_y)[:, None]
    ).astype(jnp.float32)

    def kernel(offsets_ref, wide_ref, pool_z_ref, pool_y_ref, out_ref):
        offset_value = offsets_ref[pl.program_id(0)]
        forward = margin + offset_value
        backward = margin - offset_value
        rows = []
        for block in range(blocks_x):
            total = None
            for step in range(4):
                x = block * 4 + step
                term = (
                    wide_ref[0, forward + x] * wide_ref[1, backward + x]
                    + wide_ref[2, forward + x] * wide_ref[3, backward + x]
                )
                total = term if total is None else total + term
            rows.append(total)
        pooled_x = jnp.concatenate(rows, axis=0)
        pooled_z = split_dot(pooled_x, pool_z_ref[...], True)
        pooled = split_dot(pool_y_ref[...], pooled_z, False)
        out_ref[0] = (pooled * (1.0 / 64.0)).reshape(blocks_x, blocks_y, blocks_z)

    return pl.pallas_call(
        kernel,
        grid_spec=pltpu.PrefetchScalarGridSpec(
            num_scalar_prefetch=1,
            grid=(count,),
            in_specs=[
                pl.BlockSpec((fields, span_x, size_y, size_z), lambda i, offsets_ref: (0, 0, 0, 0)),
                pl.BlockSpec((size_z, blocks_z), lambda i, offsets_ref: (0, 0)),
                pl.BlockSpec((blocks_x * blocks_y, blocks_x * size_y), lambda i, offsets_ref: (0, 0)),
            ],
            out_specs=pl.BlockSpec((1, blocks_x, blocks_y, blocks_z), lambda i, offsets_ref: (i, 0, 0, 0)),
        ),
        out_shape=jax.ShapeDtypeStruct((count, blocks_x, blocks_y, blocks_z), jnp.float32),
    )(offsets, wide, pool_z, pool_y)


def conv_apply(padded, conv_weight, conv_bias):
    channels, span_x, span_y, span_z = padded.shape
    size_x, size_y, size_z = (span_x - 2, span_y - 2, span_z - 2)
    patches = jnp.stack(
        [
            padded[:, step_x : step_x + size_x, step_y : step_y + size_y, step_z : step_z + size_z]
            for step_x in range(3)
            for step_y in range(3)
            for step_z in range(3)
        ],
        axis=1,
    )
    patches = patches.reshape(channels * 27, size_x * size_y * size_z)
    matrix = conv_weight.reshape(conv_weight.shape[0], channels * 27)
    result = jnp.dot(
        matrix, patches, precision=lax.Precision.HIGHEST, preferred_element_type=jnp.float32
    )
    result = result + conv_bias[:, None]
    return result.reshape(conv_weight.shape[0], size_x, size_y * size_z)


def group_sum_windows(coarse, axis):
    count = lax.axis_size(axis)
    rows = coarse.shape[2] // count
    rimmed = jnp.pad(coarse, ((0, 0), (0, 0), (1, 1), (0, 0)))
    windows = jnp.stack(
        [lax.slice_in_dim(rimmed, k, k + (count - 1) * rows + 1, stride=rows, axis=2) for k in range(rows + 2)]
    )
    windows = jnp.moveaxis(windows, 3, 0)
    received = lax.all_to_all(windows, axis, 0, 0, tiled=True)
    return jnp.moveaxis(received.sum(axis=0), 0, 2)


def local(
    source_prev,
    source_now,
    receiver_prev,
    receiver_now,
    courant,
    source_cells,
    wavelet,
    receiver_cells,
    receiver_data,
    offsets,
    conv_weight,
    conv_bias,
):
    cells_x, size_y, size_z = courant.shape
    slab_index = lax.axis_index("gx")
    first_x = slab_index * cells_x
    previous = jnp.stack([source_prev[0], receiver_prev[0]])
    current = jnp.stack([source_now[0], receiver_now[0]])
    current_wide, previous_wide, courant_wide = input_halo(current, previous, courant, "gx")
    levels = []
    for step_index in range(2):
        if step_index == 0:
            cells_here, first_here = cells_x + 2, first_x - 1
            step_previous, step_extended, step_courant = previous_wide, current_wide, courant_wide
        else:
            cells_here, first_here = cells_x, first_x
            step_previous, step_extended, step_courant = current, levels[0], courant
        sources = jnp.stack(
            [
                inject(cells_here, first_here, source_cells[0], wavelet[0, step_index], size_y, size_z),
                inject(
                    cells_here, first_here, receiver_cells[0], receiver_data[0, step_index], size_y, size_z
                ),
            ]
        )
        advanced = laplace_step(step_previous, step_extended, step_courant, sources)
        levels.append(advanced)
    levels[0] = levels[0][:, 1:-1]
    fields = jnp.concatenate(levels, axis=0)
    wide = padded_2(fields, (("gx", 1),), HMAX + 4)
    coarse = offset_image(wide, offsets, HMAX, cells_x + 8)
    summed = group_sum_windows(coarse, "shot")
    window = jnp.pad(summed, ((0, 0), (0, 0), (0, 0), (1, 1)))
    return conv_apply(window, conv_weight, conv_bias)


def solution(mesh):
    in_specs = (
        P("shot", "gx", None, None),
        P("shot", "gx", None, None),
        P("shot", "gx", None, None),
        P("shot", "gx", None, None),
        P("gx", None, None),
        P("shot", None),
        P("shot", None, None),
        P("shot", None),
        P("shot", None, None),
        P(),
        P(),
        P(),
    )
    out_specs = P(None, "gx", "shot")
    return jax.shard_map(local, mesh=mesh, in_specs=in_specs, out_specs=out_specs, check_vma=False)
```

```python
import jax
import jax.numpy as jnp
from jax import lax
from jax.experimental import pallas as pl
from jax.experimental.pallas import tpu as pltpu
from jax.sharding import PartitionSpec as P

HMAX = 8


def padded_2(block, sides, width):
    for axis, dim in sides:
        count = lax.axis_size(axis)
        forward = [(i, i + 1) for i in range(count - 1)]
        backward = [(target, source) for source, target in forward]
        low = lax.ppermute(
            lax.slice_in_dim(block, block.shape[dim] - width, None, axis=dim), axis, forward
        )
        high = lax.ppermute(lax.slice_in_dim(block, 0, width, axis=dim), axis, backward)
        block = jnp.concatenate([low, block, high], axis=dim)
    return block


def input_halo(current, previous, courant, axis):
    count = lax.axis_size(axis)
    forward = [(i, i + 1) for i in range(count - 1)]
    backward = [(target, source) for source, target in forward]
    fields, cells_x, size_y, size_z = current.shape

    def pack(now_planes, prev_planes, courant_planes):
        return jnp.concatenate(
            [now_planes.reshape(-1, size_y, size_z), prev_planes.reshape(-1, size_y, size_z), courant_planes]
        )

    def unpack(planes):
        now_planes = planes[: 2 * fields].reshape(fields, 2, size_y, size_z)
        prev_planes = planes[2 * fields : 3 * fields].reshape(fields, 1, size_y, size_z)
        return now_planes, prev_planes, planes[3 * fields :]

    low = lax.ppermute(
        pack(current[:, -2:], previous[:, -1:], courant[-1:]), axis, forward
    )
    high = lax.ppermute(pack(current[:, :2], previous[:, :1], courant[:1]), axis, backward)
    low_now, low_prev, low_courant = unpack(low)
    high_now, high_prev, high_courant = unpack(high)
    current_wide = jnp.concatenate([low_now, current, high_now], axis=1)
    previous_wide = jnp.concatenate([low_prev, previous, high_prev], axis=1)
    courant_wide = jnp.concatenate([low_courant, courant, high_courant], axis=0)
    return current_wide, previous_wide, courant_wide


def bf16_parts(value):
    high = value.astype(jnp.bfloat16)
    rest = value - high.astype(jnp.float32)
    middle = rest.astype(jnp.bfloat16)
    low = (rest - middle.astype(jnp.float32)).astype(jnp.bfloat16)
    return (high, middle, low)


def rounded_parts(value):
    high = lax.reduce_precision(value, exponent_bits=8, mantissa_bits=7)
    rest = value - high
    middle = lax.reduce_precision(rest, exponent_bits=8, mantissa_bits=7)
    low = rest - middle
    return (high.astype(jnp.bfloat16), middle.astype(jnp.bfloat16), low.astype(jnp.bfloat16))


def inject(cells_here, first_x, cell_index, amplitudes, size_y, size_z):
    plane_size = size_y * size_z
    column = cell_index // plane_size
    within = cell_index % plane_size
    row = (column - first_x) * size_y + within // size_z
    rows = (jnp.arange(cells_here * size_y)[:, None] == row[None, :]).astype(jnp.bfloat16)
    at_z = jnp.arange(size_z)[None, :] == (within % size_z)[:, None]
    fields = []
    for amplitude in amplitudes:
        placed = jnp.where(at_z, amplitude[:, None], 0.0)
        parts = jnp.concatenate(rounded_parts(placed), axis=1)
        sums = jnp.dot(rows, parts, preferred_element_type=jnp.float32)
        total = sums[:, :size_z] + sums[:, size_z : 2 * size_z] + sums[:, 2 * size_z :]
        fields.append(total.reshape(cells_here, size_y, size_z))
    return fields


def laplace_step(previous, extended, courant, sources):
    center = extended[:, 1:-1]
    padded = jnp.pad(center, ((0, 0), (0, 0), (1, 1), (1, 1)))
    laplace = extended[:, 2:] + extended[:, :-2]
    laplace = laplace + padded[:, :, 2:, 1:-1] + padded[:, :, :-2, 1:-1]
    laplace = laplace + padded[:, :, 1:-1, 2:] + padded[:, :, 1:-1, :-2] - 6.0 * center
    return 2.0 * center - previous + courant * laplace + sources


def pooling(size, group):
    fine = jnp.arange(size)[:, None] // group
    coarse = jnp.arange(size // group)[None, :]
    return (fine == coarse).astype(jnp.float32)


def split_dot(left, right, split_left):
    total = None
    if split_left:
        pieces = [(piece, right.astype(jnp.bfloat16)) for piece in bf16_parts(left)]
    else:
        pieces = [(left.astype(jnp.bfloat16), piece) for piece in bf16_parts(right)]
    for a, b in pieces:
        term = jnp.dot(a, b, preferred_element_type=jnp.float32)
        total = term if total is None else total + term
    return total


def offset_image(wide, offsets, margin, cells_x):
    fields, span_x, size_y, size_z = wide.shape
    count = offsets.shape[0]
    blocks_x, blocks_y, blocks_z = cells_x // 4, size_y // 4, size_z // 4
    pool_z = pooling(size_z, 4)
    pool_y = (
        (jnp.arange(blocks_x * size_y)[None, :] // 4) == jnp.arange(blocks_x * blocks_y)[:, None]
    ).astype(jnp.float32)

    def kernel(offsets_ref, wide_ref, pool_z_ref, pool_y_ref, out_ref):
        def per_offset(index, carry):
            offset_value = offsets_ref[index]
            forward = margin + offset_value
            backward = margin - offset_value
            rows = []
            for block in range(blocks_x):
                total = None
                for step in range(4):
                    x = block * 4 + step
                    term = (
                        wide_ref[0, forward + x] * wide_ref[1, backward + x]
                        + wide_ref[2, forward + x] * wide_ref[3, backward + x]
                    )
                    total = term if total is None else total + term
                rows.append(total)
            pooled_x = jnp.concatenate(rows, axis=0)
            pooled_z = split_dot(pooled_x, pool_z_ref[...], True)
            pooled = split_dot(pool_y_ref[...], pooled_z, False)
            out_ref[index] = (pooled * (1.0 / 64.0)).reshape(blocks_x, blocks_y, blocks_z)
            return carry

        lax.fori_loop(0, count, per_offset, 0)

    return pl.pallas_call(
        kernel,
        grid_spec=pltpu.PrefetchScalarGridSpec(
            num_scalar_prefetch=1,
            grid=(1,),
            in_specs=[
                pl.BlockSpec((fields, span_x, size_y, size_z), lambda i, offsets_ref: (0, 0, 0, 0)),
                pl.BlockSpec((size_z, blocks_z), lambda i, offsets_ref: (0, 0)),
                pl.BlockSpec((blocks_x * blocks_y, blocks_x * size_y), lambda i, offsets_ref: (0, 0)),
            ],
            out_specs=pl.BlockSpec((count, blocks_x, blocks_y, blocks_z), lambda i, offsets_ref: (0, 0, 0, 0)),
        ),
        out_shape=jax.ShapeDtypeStruct((count, blocks_x, blocks_y, blocks_z), jnp.float32),
    )(offsets, wide, pool_z, pool_y)


def conv_apply(padded, conv_weight, conv_bias):
    channels, span_x, span_y, span_z = padded.shape
    size_x, size_y, size_z = (span_x - 2, span_y - 2, span_z - 2)
    patches = jnp.stack(
        [
            padded[:, step_x : step_x + size_x, step_y : step_y + size_y, step_z : step_z + size_z]
            for step_x in range(3)
            for step_y in range(3)
            for step_z in range(3)
        ],
        axis=1,
    )
    patches = patches.reshape(channels * 27, size_x * size_y * size_z)
    matrix = conv_weight.reshape(conv_weight.shape[0], channels * 27)
    result = jnp.dot(
        matrix, patches, precision=lax.Precision.HIGHEST, preferred_element_type=jnp.float32
    )
    result = result + conv_bias[:, None]
    return result.reshape(conv_weight.shape[0], size_x, size_y * size_z)


def group_sum_windows(coarse, axis):
    count = lax.axis_size(axis)
    rows = coarse.shape[2] // count
    rimmed = jnp.pad(coarse, ((0, 0), (0, 0), (1, 1), (0, 0)))
    windows = jnp.stack(
        [lax.slice_in_dim(rimmed, k, k + (count - 1) * rows + 1, stride=rows, axis=2) for k in range(rows + 2)]
    )
    windows = jnp.moveaxis(windows, 3, 0)
    received = lax.all_to_all(windows, axis, 0, 0, tiled=True)
    return jnp.moveaxis(received.sum(axis=0), 0, 2)


def local(
    source_prev,
    source_now,
    receiver_prev,
    receiver_now,
    courant,
    source_cells,
    wavelet,
    receiver_cells,
    receiver_data,
    offsets,
    conv_weight,
    conv_bias,
):
    cells_x, size_y, size_z = courant.shape
    slab_index = lax.axis_index("gx")
    first_x = slab_index * cells_x
    previous = jnp.stack([source_prev[0], receiver_prev[0]])
    current = jnp.stack([source_now[0], receiver_now[0]])
    current_wide, previous_wide, courant_wide = input_halo(current, previous, courant, "gx")
    source_fields = inject(cells_x + 2, first_x - 1, source_cells[0], wavelet[0], size_y, size_z)
    receiver_fields = inject(cells_x + 2, first_x - 1, receiver_cells[0], receiver_data[0], size_y, size_z)
    levels = []
    for step_index in range(2):
        sources = jnp.stack([source_fields[step_index], receiver_fields[step_index]])
        if step_index == 0:
            step_previous, step_extended, step_courant = previous_wide, current_wide, courant_wide
        else:
            sources = sources[:, 1:-1]
            step_previous, step_extended, step_courant = current, levels[0], courant
        advanced = laplace_step(step_previous, step_extended, step_courant, sources)
        levels.append(advanced)
    levels[0] = levels[0][:, 1:-1]
    fields = jnp.concatenate(levels, axis=0)
    wide = padded_2(fields, (("gx", 1),), HMAX + 4)
    coarse = offset_image(wide, offsets, HMAX, cells_x + 8)
    summed = group_sum_windows(coarse, "shot")
    window = jnp.pad(summed, ((0, 0), (0, 0), (0, 0), (1, 1)))
    return conv_apply(window, conv_weight, conv_bias)


def solution(mesh):
    in_specs = (
        P("shot", "gx", None, None),
        P("shot", "gx", None, None),
        P("shot", "gx", None, None),
        P("shot", "gx", None, None),
        P("gx", None, None),
        P("shot", None),
        P("shot", None, None),
        P("shot", None),
        P("shot", None, None),
        P(),
        P(),
        P(),
    )
    out_specs = P(None, "gx", "shot")
    return jax.shard_map(local, mesh=mesh, in_specs=in_specs, out_specs=out_specs, check_vma=False)
```

```python
import jax
import jax.numpy as jnp
from jax import lax
from jax.experimental import pallas as pl
from jax.experimental.pallas import tpu as pltpu
from jax.sharding import PartitionSpec as P

HMAX = 8


def padded_2(block, sides, width):
    for axis, dim in sides:
        count = lax.axis_size(axis)
        forward = [(i, i + 1) for i in range(count - 1)]
        backward = [(target, source) for source, target in forward]
        low = lax.ppermute(
            lax.slice_in_dim(block, block.shape[dim] - width, None, axis=dim), axis, forward
        )
        high = lax.ppermute(lax.slice_in_dim(block, 0, width, axis=dim), axis, backward)
        block = jnp.concatenate([low, block, high], axis=dim)
    return block


def halo_pieces(block, axis, width):
    count = lax.axis_size(axis)
    forward = [(i, i + 1) for i in range(count - 1)]
    backward = [(target, source) for source, target in forward]
    low = lax.ppermute(block[:, block.shape[1] - width :], axis, forward)
    high = lax.ppermute(block[:, :width], axis, backward)
    return [low, block, high]


def input_halo(current, previous, courant, axis):
    count = lax.axis_size(axis)
    forward = [(i, i + 1) for i in range(count - 1)]
    backward = [(target, source) for source, target in forward]
    fields, cells_x, size_y, size_z = current.shape

    def pack(now_planes, prev_planes, courant_planes):
        return jnp.concatenate(
            [now_planes.reshape(-1, size_y, size_z), prev_planes.reshape(-1, size_y, size_z), courant_planes]
        )

    def unpack(planes):
        now_planes = planes[: 2 * fields].reshape(fields, 2, size_y, size_z)
        prev_planes = planes[2 * fields : 3 * fields].reshape(fields, 1, size_y, size_z)
        return now_planes, prev_planes, planes[3 * fields :]

    low = lax.ppermute(
        pack(current[:, -2:], previous[:, -1:], courant[-1:]), axis, forward
    )
    high = lax.ppermute(pack(current[:, :2], previous[:, :1], courant[:1]), axis, backward)
    low_now, low_prev, low_courant = unpack(low)
    high_now, high_prev, high_courant = unpack(high)
    current_wide = jnp.concatenate([low_now, current, high_now], axis=1)
    previous_wide = jnp.concatenate([low_prev, previous, high_prev], axis=1)
    courant_wide = jnp.concatenate([low_courant, courant, high_courant], axis=0)
    return current_wide, previous_wide, courant_wide


def bf16_parts(value):
    high = value.astype(jnp.bfloat16)
    rest = value - high.astype(jnp.float32)
    middle = rest.astype(jnp.bfloat16)
    low = (rest - middle.astype(jnp.float32)).astype(jnp.bfloat16)
    return (high, middle, low)


def rounded_parts(value):
    high = lax.reduce_precision(value, exponent_bits=8, mantissa_bits=7)
    rest = value - high
    middle = lax.reduce_precision(rest, exponent_bits=8, mantissa_bits=7)
    low = rest - middle
    return (high.astype(jnp.bfloat16), middle.astype(jnp.bfloat16), low.astype(jnp.bfloat16))


def inject(cells_here, first_x, cell_index, amplitudes, size_y, size_z):
    plane_size = size_y * size_z
    column = cell_index // plane_size
    within = cell_index % plane_size
    row = (column - first_x) * size_y + within // size_z
    rows = (jnp.arange(cells_here * size_y)[:, None] == row[None, :]).astype(jnp.bfloat16)
    at_z = jnp.arange(size_z)[None, :] == (within % size_z)[:, None]
    fields = []
    for amplitude in amplitudes:
        placed = jnp.where(at_z, amplitude[:, None], 0.0)
        parts = jnp.concatenate(rounded_parts(placed), axis=1)
        sums = jnp.dot(rows, parts, preferred_element_type=jnp.float32)
        total = sums[:, :size_z] + sums[:, size_z : 2 * size_z] + sums[:, 2 * size_z :]
        fields.append(total.reshape(cells_here, size_y, size_z))
    return fields


def laplace_step(previous, extended, courant, sources):
    center = extended[:, 1:-1]
    padded = jnp.pad(center, ((0, 0), (0, 0), (1, 1), (1, 1)))
    laplace = extended[:, 2:] + extended[:, :-2]
    laplace = laplace + padded[:, :, 2:, 1:-1] + padded[:, :, :-2, 1:-1]
    laplace = laplace + padded[:, :, 1:-1, 2:] + padded[:, :, 1:-1, :-2] - 6.0 * center
    return 2.0 * center - previous + courant * laplace + sources


def pooling(size, group):
    fine = jnp.arange(size)[:, None] // group
    coarse = jnp.arange(size // group)[None, :]
    return (fine == coarse).astype(jnp.float32)


def split_dot(left, right, split_left):
    total = None
    if split_left:
        pieces = [(piece, right.astype(jnp.bfloat16)) for piece in bf16_parts(left)]
    else:
        pieces = [(left.astype(jnp.bfloat16), piece) for piece in bf16_parts(right)]
    for a, b in pieces:
        term = jnp.dot(a, b, preferred_element_type=jnp.float32)
        total = term if total is None else total + term
    return total


def offset_image(pieces, offsets, margin, cells_x):
    fields, _, size_y, size_z = pieces[0].shape
    spans = [piece.shape[1] for piece in pieces]
    starts = [sum(spans[:k]) for k in range(len(spans))]
    span_x = sum(spans)
    count = offsets.shape[0]
    blocks_x, blocks_y, blocks_z = cells_x // 4, size_y // 4, size_z // 4
    pool_z = pooling(size_z, 4)

    def kernel(offsets_ref, *refs):
        piece_refs = refs[: len(pieces)]
        pool_z_ref, out_ref, wide_ref, sum_ref, semaphores = refs[len(pieces) :]
        copies = [
            pltpu.make_async_copy(piece_ref, wide_ref.at[:, start : start + span], semaphores.at[k])
            for k, (piece_ref, start, span) in enumerate(zip(piece_refs, starts, spans))
        ]
        for copy in copies:
            copy.start()
        for copy in copies:
            copy.wait()

        def per_offset(index, carry):
            offset_value = offsets_ref[index]
            forward = margin + offset_value
            backward = margin - offset_value
            for block in range(blocks_x):
                total = None
                for step in range(4):
                    x = block * 4 + step
                    term = (
                        wide_ref[0, forward + x] * wide_ref[1, backward + x]
                        + wide_ref[2, forward + x] * wide_ref[3, backward + x]
                    )
                    total = term if total is None else total + term
                sum_ref[block * size_y : (block + 1) * size_y, :] = total
            pooled_y = None
            for step in range(4):
                rows = sum_ref[pl.ds(step, blocks_x * blocks_y, stride=4), :]
                pooled_y = rows if pooled_y is None else pooled_y + rows
            pooled = split_dot(pooled_y, pool_z_ref[...], True)
            out_ref[index] = (pooled * (1.0 / 64.0)).reshape(blocks_x, blocks_y, blocks_z)
            return carry

        lax.fori_loop(0, count, per_offset, 0)

    return pl.pallas_call(
        kernel,
        grid_spec=pltpu.PrefetchScalarGridSpec(
            num_scalar_prefetch=1,
            grid=(1,),
            in_specs=[pl.BlockSpec(memory_space=pl.ANY) for _ in pieces]
            + [pl.BlockSpec((size_z, blocks_z), lambda i, offsets_ref: (0, 0))],
            out_specs=pl.BlockSpec((count, blocks_x, blocks_y, blocks_z), lambda i, offsets_ref: (0, 0, 0, 0)),
            scratch_shapes=[
                pltpu.VMEM((fields, span_x, size_y, size_z), jnp.float32),
                pltpu.VMEM((blocks_x * size_y, size_z), jnp.float32),
                pltpu.SemaphoreType.DMA((len(pieces),)),
            ],
        ),
        out_shape=jax.ShapeDtypeStruct((count, blocks_x, blocks_y, blocks_z), jnp.float32),
    )(offsets, *pieces, pool_z)


def conv_apply(padded, conv_weight, conv_bias):
    channels, span_x, span_y, span_z = padded.shape
    size_x, size_y, size_z = (span_x - 2, span_y - 2, span_z - 2)
    patches = jnp.stack(
        [
            padded[:, step_x : step_x + size_x, step_y : step_y + size_y, step_z : step_z + size_z]
            for step_x in range(3)
            for step_y in range(3)
            for step_z in range(3)
        ],
        axis=1,
    )
    patches = patches.reshape(channels * 27, size_x * size_y * size_z)
    matrix = conv_weight.reshape(conv_weight.shape[0], channels * 27)
    result = jnp.dot(
        matrix, patches, precision=lax.Precision.HIGHEST, preferred_element_type=jnp.float32
    )
    result = result + conv_bias[:, None]
    return result.reshape(conv_weight.shape[0], size_x, size_y * size_z)


def group_sum_windows(coarse, axis):
    count = lax.axis_size(axis)
    rows = coarse.shape[2] // count
    rimmed = jnp.pad(coarse, ((0, 0), (0, 0), (1, 1), (0, 0)))
    windows = jnp.stack(
        [lax.slice_in_dim(rimmed, k, k + (count - 1) * rows + 1, stride=rows, axis=2) for k in range(rows + 2)]
    )
    windows = jnp.moveaxis(windows, 3, 0)
    received = lax.all_to_all(windows, axis, 0, 0, tiled=True)
    return jnp.moveaxis(received.sum(axis=0), 0, 2)


def local(
    source_prev,
    source_now,
    receiver_prev,
    receiver_now,
    courant,
    source_cells,
    wavelet,
    receiver_cells,
    receiver_data,
    offsets,
    conv_weight,
    conv_bias,
):
    cells_x, size_y, size_z = courant.shape
    slab_index = lax.axis_index("gx")
    first_x = slab_index * cells_x
    previous = jnp.stack([source_prev[0], receiver_prev[0]])
    current = jnp.stack([source_now[0], receiver_now[0]])
    current_wide, previous_wide, courant_wide = input_halo(current, previous, courant, "gx")
    source_fields = inject(cells_x + 2, first_x - 1, source_cells[0], wavelet[0], size_y, size_z)
    receiver_fields = inject(cells_x + 2, first_x - 1, receiver_cells[0], receiver_data[0], size_y, size_z)
    levels = []
    for step_index in range(2):
        sources = jnp.stack([source_fields[step_index], receiver_fields[step_index]])
        if step_index == 0:
            step_previous, step_extended, step_courant = previous_wide, current_wide, courant_wide
        else:
            sources = sources[:, 1:-1]
            step_previous, step_extended, step_courant = current, levels[0], courant
        advanced = laplace_step(step_previous, step_extended, step_courant, sources)
        levels.append(advanced)
    levels[0] = levels[0][:, 1:-1]
    fields = jnp.concatenate(levels, axis=0)
    coarse = offset_image(halo_pieces(fields, "gx", HMAX + 4), offsets, HMAX, cells_x + 8)
    summed = group_sum_windows(coarse, "shot")
    window = jnp.pad(summed, ((0, 0), (0, 0), (0, 0), (1, 1)))
    return conv_apply(window, conv_weight, conv_bias)


def solution(mesh):
    in_specs = (
        P("shot", "gx", None, None),
        P("shot", "gx", None, None),
        P("shot", "gx", None, None),
        P("shot", "gx", None, None),
        P("gx", None, None),
        P("shot", None),
        P("shot", None, None),
        P("shot", None),
        P("shot", None, None),
        P(),
        P(),
        P(),
    )
    out_specs = P(None, "gx", "shot")
    return jax.shard_map(local, mesh=mesh, in_specs=in_specs, out_specs=out_specs, check_vma=False)
```

```python
import jax
import jax.numpy as jnp
from jax import lax
from jax.experimental import pallas as pl
from jax.experimental.pallas import tpu as pltpu
from jax.sharding import PartitionSpec as P

HMAX = 8


def padded_2(block, sides, width):
    for axis, dim in sides:
        count = lax.axis_size(axis)
        forward = [(i, i + 1) for i in range(count - 1)]
        backward = [(target, source) for source, target in forward]
        low = lax.ppermute(
            lax.slice_in_dim(block, block.shape[dim] - width, None, axis=dim), axis, forward
        )
        high = lax.ppermute(lax.slice_in_dim(block, 0, width, axis=dim), axis, backward)
        block = jnp.concatenate([low, block, high], axis=dim)
    return block


def halo_pieces(block, axis, width):
    count = lax.axis_size(axis)
    forward = [(i, i + 1) for i in range(count - 1)]
    backward = [(target, source) for source, target in forward]
    low = lax.ppermute(block[:, block.shape[1] - width :], axis, forward)
    high = lax.ppermute(block[:, :width], axis, backward)
    return low, high


def input_halo(current, previous, courant, axis):
    count = lax.axis_size(axis)
    forward = [(i, i + 1) for i in range(count - 1)]
    backward = [(target, source) for source, target in forward]
    fields, cells_x, size_y, size_z = current.shape

    def pack(now_planes, prev_planes, courant_planes):
        return jnp.concatenate(
            [now_planes.reshape(-1, size_y, size_z), prev_planes.reshape(-1, size_y, size_z), courant_planes]
        )

    def unpack(planes):
        now_planes = planes[: 2 * fields].reshape(fields, 2, size_y, size_z)
        prev_planes = planes[2 * fields : 3 * fields].reshape(fields, 1, size_y, size_z)
        return now_planes, prev_planes, planes[3 * fields :]

    low = lax.ppermute(
        pack(current[:, -2:], previous[:, -1:], courant[-1:]), axis, forward
    )
    high = lax.ppermute(pack(current[:, :2], previous[:, :1], courant[:1]), axis, backward)
    low_now, low_prev, low_courant = unpack(low)
    high_now, high_prev, high_courant = unpack(high)
    current_wide = jnp.concatenate([low_now, current, high_now], axis=1)
    previous_wide = jnp.concatenate([low_prev, previous, high_prev], axis=1)
    courant_wide = jnp.concatenate([low_courant, courant, high_courant], axis=0)
    return current_wide, previous_wide, courant_wide


def bf16_parts(value):
    high = value.astype(jnp.bfloat16)
    rest = value - high.astype(jnp.float32)
    middle = rest.astype(jnp.bfloat16)
    low = (rest - middle.astype(jnp.float32)).astype(jnp.bfloat16)
    return (high, middle, low)


def rounded_parts(value):
    high = lax.reduce_precision(value, exponent_bits=8, mantissa_bits=7)
    rest = value - high
    middle = lax.reduce_precision(rest, exponent_bits=8, mantissa_bits=7)
    low = rest - middle
    return (high.astype(jnp.bfloat16), middle.astype(jnp.bfloat16), low.astype(jnp.bfloat16))


def inject(cells_here, first_x, cell_index, amplitudes, size_y, size_z):
    plane_size = size_y * size_z
    column = cell_index // plane_size
    within = cell_index % plane_size
    row = (column - first_x) * size_y + within // size_z
    rows = (jnp.arange(cells_here * size_y)[:, None] == row[None, :]).astype(jnp.bfloat16)
    at_z = jnp.arange(size_z)[None, :] == (within % size_z)[:, None]
    fields = []
    for amplitude in amplitudes:
        placed = jnp.where(at_z, amplitude[:, None], 0.0)
        parts = jnp.concatenate(rounded_parts(placed), axis=1)
        sums = jnp.dot(rows, parts, preferred_element_type=jnp.float32)
        total = sums[:, :size_z] + sums[:, size_z : 2 * size_z] + sums[:, 2 * size_z :]
        fields.append(total.reshape(cells_here, size_y, size_z))
    return fields


def laplace_step(previous, extended, courant, sources):
    center = extended[:, 1:-1]
    padded = jnp.pad(center, ((0, 0), (0, 0), (1, 1), (1, 1)))
    laplace = extended[:, 2:] + extended[:, :-2]
    laplace = laplace + padded[:, :, 2:, 1:-1] + padded[:, :, :-2, 1:-1]
    laplace = laplace + padded[:, :, 1:-1, 2:] + padded[:, :, 1:-1, :-2] - 6.0 * center
    return 2.0 * center - previous + courant * laplace + sources


def pooling(size, group):
    fine = jnp.arange(size)[:, None] // group
    coarse = jnp.arange(size // group)[None, :]
    return (fine == coarse).astype(jnp.float32)


def split_dot(left, right, split_left):
    total = None
    if split_left:
        pieces = [(piece, right.astype(jnp.bfloat16)) for piece in bf16_parts(left)]
    else:
        pieces = [(left.astype(jnp.bfloat16), piece) for piece in bf16_parts(right)]
    for a, b in pieces:
        term = jnp.dot(a, b, preferred_element_type=jnp.float32)
        total = term if total is None else total + term
    return total


def offset_image(pieces, offsets, margin, cells_x):
    size_y, size_z = pieces[0][0].shape[2:]
    fields = max(first + array.shape[0] for array, first, _, _, _ in pieces)
    span_x = max(at + span for _, _, at, _, span in pieces)
    count = offsets.shape[0]
    blocks_x, blocks_y, blocks_z = cells_x // 4, size_y // 4, size_z // 4
    pool_z = pooling(size_z, 4)

    def kernel(offsets_ref, *refs):
        piece_refs = refs[: len(pieces)]
        pool_z_ref, out_ref, wide_ref, sum_ref, semaphores = refs[len(pieces) :]
        copies = []
        for k, (piece_ref, (array, first, at, taken, span)) in enumerate(zip(piece_refs, pieces)):
            source = piece_ref.at[:, taken : taken + span] if span != array.shape[1] else piece_ref
            target = wide_ref.at[first : first + array.shape[0], at : at + span]
            copies.append(pltpu.make_async_copy(source, target, semaphores.at[k]))
        for copy in copies:
            copy.start()
        for copy in copies:
            copy.wait()

        def per_offset(index, carry):
            offset_value = offsets_ref[index]
            forward = margin + offset_value
            backward = margin - offset_value
            for block in range(blocks_x):
                total = None
                for step in range(4):
                    x = block * 4 + step
                    term = (
                        wide_ref[0, forward + x] * wide_ref[1, backward + x]
                        + wide_ref[2, forward + x] * wide_ref[3, backward + x]
                    )
                    total = term if total is None else total + term
                sum_ref[block * size_y : (block + 1) * size_y, :] = total
            pooled_y = None
            for step in range(4):
                rows = sum_ref[pl.ds(step, blocks_x * blocks_y, stride=4), :]
                pooled_y = rows if pooled_y is None else pooled_y + rows
            pooled = split_dot(pooled_y, pool_z_ref[...], True)
            out_ref[index] = (pooled * (1.0 / 64.0)).reshape(blocks_x, blocks_y, blocks_z)
            return carry

        lax.fori_loop(0, count, per_offset, 0)

    return pl.pallas_call(
        kernel,
        grid_spec=pltpu.PrefetchScalarGridSpec(
            num_scalar_prefetch=1,
            grid=(1,),
            in_specs=[pl.BlockSpec(memory_space=pl.ANY) for _ in pieces]
            + [pl.BlockSpec((size_z, blocks_z), lambda i, offsets_ref: (0, 0))],
            out_specs=pl.BlockSpec((count, blocks_x, blocks_y, blocks_z), lambda i, offsets_ref: (0, 0, 0, 0)),
            scratch_shapes=[
                pltpu.VMEM((fields, span_x, size_y, size_z), jnp.float32),
                pltpu.VMEM((blocks_x * size_y, size_z), jnp.float32),
                pltpu.SemaphoreType.DMA((len(pieces),)),
            ],
        ),
        out_shape=jax.ShapeDtypeStruct((count, blocks_x, blocks_y, blocks_z), jnp.float32),
    )(offsets, *[piece[0] for piece in pieces], pool_z)


def conv_apply(padded, conv_weight, conv_bias):
    channels, span_x, span_y, span_z = padded.shape
    size_x, size_y, size_z = (span_x - 2, span_y - 2, span_z - 2)
    patches = jnp.stack(
        [
            padded[:, step_x : step_x + size_x, step_y : step_y + size_y, step_z : step_z + size_z]
            for step_x in range(3)
            for step_y in range(3)
            for step_z in range(3)
        ],
        axis=1,
    )
    patches = patches.reshape(channels * 27, size_x * size_y * size_z)
    matrix = conv_weight.reshape(conv_weight.shape[0], channels * 27)
    result = jnp.dot(
        matrix, patches, precision=lax.Precision.HIGHEST, preferred_element_type=jnp.float32
    )
    result = result + conv_bias[:, None]
    return result.reshape(conv_weight.shape[0], size_x, size_y * size_z)


def group_sum_windows(coarse, axis):
    count = lax.axis_size(axis)
    rows = coarse.shape[2] // count
    rimmed = jnp.pad(coarse, ((0, 0), (0, 0), (1, 1), (0, 0)))
    windows = jnp.stack(
        [lax.slice_in_dim(rimmed, k, k + (count - 1) * rows + 1, stride=rows, axis=2) for k in range(rows + 2)]
    )
    windows = jnp.moveaxis(windows, 3, 0)
    shape = windows.shape[1:]
    received = lax.all_to_all(windows.reshape(count, -1), axis, 0, 0, tiled=True)
    return jnp.moveaxis(received.sum(axis=0).reshape(shape), 0, 2)


def local(
    source_prev,
    source_now,
    receiver_prev,
    receiver_now,
    courant,
    source_cells,
    wavelet,
    receiver_cells,
    receiver_data,
    offsets,
    conv_weight,
    conv_bias,
):
    cells_x, size_y, size_z = courant.shape
    slab_index = lax.axis_index("gx")
    first_x = slab_index * cells_x
    previous = jnp.stack([source_prev[0], receiver_prev[0]])
    current = jnp.stack([source_now[0], receiver_now[0]])
    current_wide, previous_wide, courant_wide = input_halo(current, previous, courant, "gx")
    source_fields = inject(cells_x + 2, first_x - 1, source_cells[0], wavelet[0], size_y, size_z)
    receiver_fields = inject(cells_x + 2, first_x - 1, receiver_cells[0], receiver_data[0], size_y, size_z)
    levels = []
    for step_index in range(2):
        sources = jnp.stack([source_fields[step_index], receiver_fields[step_index]])
        if step_index == 0:
            step_previous, step_extended, step_courant = previous_wide, current_wide, courant_wide
        else:
            sources = sources[:, 1:-1]
            step_previous, step_extended, step_courant = current, levels[0], courant
        advanced = laplace_step(step_previous, step_extended, step_courant, sources)
        levels.append(advanced)
    levels_full = list(levels)
    levels[0] = levels[0][:, 1:-1]
    fields = jnp.concatenate(levels, axis=0)
    width = HMAX + 4
    low, high = halo_pieces(fields, "gx", width)
    pieces = [
        (low, 0, 0, 0, width),
        (levels_full[0], 0, width, 1, cells_x),
        (levels_full[1], 2, width, 0, cells_x),
        (high, 0, width + cells_x, 0, width),
    ]
    coarse = offset_image(pieces, offsets, HMAX, cells_x + 8)
    summed = group_sum_windows(coarse, "shot")
    window = jnp.pad(summed, ((0, 0), (0, 0), (0, 0), (1, 1)))
    return conv_apply(window, conv_weight, conv_bias)


def solution(mesh):
    in_specs = (
        P("shot", "gx", None, None),
        P("shot", "gx", None, None),
        P("shot", "gx", None, None),
        P("shot", "gx", None, None),
        P("gx", None, None),
        P("shot", None),
        P("shot", None, None),
        P("shot", None),
        P("shot", None, None),
        P(),
        P(),
        P(),
    )
    out_specs = P(None, "gx", "shot")
    return jax.shard_map(local, mesh=mesh, in_specs=in_specs, out_specs=out_specs, check_vma=False)
```

```python
import jax
import jax.numpy as jnp
from jax import lax
from jax.experimental import pallas as pl
from jax.experimental.pallas import tpu as pltpu
from jax.sharding import PartitionSpec as P

HMAX = 8


def padded_2(block, sides, width):
    for axis, dim in sides:
        count = lax.axis_size(axis)
        forward = [(i, i + 1) for i in range(count - 1)]
        backward = [(target, source) for source, target in forward]
        low = lax.ppermute(
            lax.slice_in_dim(block, block.shape[dim] - width, None, axis=dim), axis, forward
        )
        high = lax.ppermute(lax.slice_in_dim(block, 0, width, axis=dim), axis, backward)
        block = jnp.concatenate([low, block, high], axis=dim)
    return block


def halo_pieces(block, axis, width):
    count = lax.axis_size(axis)
    forward = [(i, i + 1) for i in range(count - 1)]
    backward = [(target, source) for source, target in forward]
    low = lax.ppermute(block[:, block.shape[1] - width :], axis, forward)
    high = lax.ppermute(block[:, :width], axis, backward)
    return low, high


def input_halo(current, previous, courant, axis):
    count = lax.axis_size(axis)
    forward = [(i, i + 1) for i in range(count - 1)]
    backward = [(target, source) for source, target in forward]
    fields, cells_x, size_y, size_z = current.shape

    def pack(now_planes, prev_planes, courant_planes):
        return jnp.concatenate(
            [now_planes.reshape(-1, size_y, size_z), prev_planes.reshape(-1, size_y, size_z), courant_planes]
        )

    def unpack(planes):
        now_planes = planes[: 2 * fields].reshape(fields, 2, size_y, size_z)
        prev_planes = planes[2 * fields : 3 * fields].reshape(fields, 1, size_y, size_z)
        return now_planes, prev_planes, planes[3 * fields :]

    low = lax.ppermute(
        pack(current[:, -2:], previous[:, -1:], courant[-1:]), axis, forward
    )
    high = lax.ppermute(pack(current[:, :2], previous[:, :1], courant[:1]), axis, backward)
    low_now, low_prev, low_courant = unpack(low)
    high_now, high_prev, high_courant = unpack(high)
    current_wide = jnp.concatenate([low_now, current, high_now], axis=1)
    previous_wide = jnp.concatenate([low_prev, previous, high_prev], axis=1)
    courant_wide = jnp.concatenate([low_courant, courant, high_courant], axis=0)
    return current_wide, previous_wide, courant_wide


def bf16_parts(value):
    high = value.astype(jnp.bfloat16)
    rest = value - high.astype(jnp.float32)
    middle = rest.astype(jnp.bfloat16)
    low = (rest - middle.astype(jnp.float32)).astype(jnp.bfloat16)
    return (high, middle, low)


def rounded_parts(value):
    high = lax.reduce_precision(value, exponent_bits=8, mantissa_bits=7)
    rest = value - high
    middle = lax.reduce_precision(rest, exponent_bits=8, mantissa_bits=7)
    low = rest - middle
    return (high.astype(jnp.bfloat16), middle.astype(jnp.bfloat16), low.astype(jnp.bfloat16))


def inject(cells_here, first_x, cell_index, amplitudes, size_y, size_z):
    plane_size = size_y * size_z
    column = cell_index // plane_size
    within = cell_index % plane_size
    row = (column - first_x) * size_y + within // size_z
    rows = (jnp.arange(cells_here * size_y)[:, None] == row[None, :]).astype(jnp.bfloat16)
    at_z = jnp.arange(size_z)[None, :] == (within % size_z)[:, None]
    fields = []
    for amplitude in amplitudes:
        placed = jnp.where(at_z, amplitude[:, None], 0.0)
        parts = jnp.concatenate(rounded_parts(placed), axis=1)
        sums = jnp.dot(rows, parts, preferred_element_type=jnp.float32)
        total = sums[:, :size_z] + sums[:, size_z : 2 * size_z] + sums[:, 2 * size_z :]
        fields.append(total.reshape(cells_here, size_y, size_z))
    return fields


def laplace_step(previous, extended, courant, sources):
    center = extended[:, 1:-1]
    padded = jnp.pad(center, ((0, 0), (0, 0), (1, 1), (1, 1)))
    laplace = extended[:, 2:] + extended[:, :-2]
    laplace = laplace + padded[:, :, 2:, 1:-1] + padded[:, :, :-2, 1:-1]
    laplace = laplace + padded[:, :, 1:-1, 2:] + padded[:, :, 1:-1, :-2] - 6.0 * center
    return 2.0 * center - previous + courant * laplace + sources


def pooling(size, group):
    fine = jnp.arange(size)[:, None] // group
    coarse = jnp.arange(size // group)[None, :]
    return (fine == coarse).astype(jnp.float32)


def split_dot(left, right, split_left):
    total = None
    if split_left:
        pieces = [(piece, right.astype(jnp.bfloat16)) for piece in bf16_parts(left)]
    else:
        pieces = [(left.astype(jnp.bfloat16), piece) for piece in bf16_parts(right)]
    for a, b in pieces:
        term = jnp.dot(a, b, preferred_element_type=jnp.float32)
        total = term if total is None else total + term
    return total


def offset_image(pieces, offsets, margin, cells_x):
    size_y, size_z = pieces[0][0].shape[2:]
    fields = max(first + array.shape[0] for array, first, _, _, _ in pieces)
    span_x = max(at + span for _, _, at, _, span in pieces)
    count = offsets.shape[0]
    blocks_x, blocks_y, blocks_z = cells_x // 4, size_y // 4, size_z // 4
    pool_z = pooling(size_z, 4)

    def kernel(offsets_ref, *refs):
        piece_refs = refs[: len(pieces)]
        pool_z_ref, out_ref, wide_ref, sum_ref, semaphores = refs[len(pieces) :]
        copies = []
        for k, (piece_ref, (array, first, at, taken, span)) in enumerate(zip(piece_refs, pieces)):
            source = piece_ref.at[:, taken : taken + span] if span != array.shape[1] else piece_ref
            target = wide_ref.at[first : first + array.shape[0], at : at + span]
            copies.append(pltpu.make_async_copy(source, target, semaphores.at[k]))
        for copy in copies:
            copy.start()
        for copy in copies:
            copy.wait()

        def per_offset(index, carry):
            offset_value = offsets_ref[index]
            forward = margin + offset_value
            backward = margin - offset_value
            for block in range(blocks_x):
                total = None
                for step in range(4):
                    x = block * 4 + step
                    term = (
                        wide_ref[0, forward + x] * wide_ref[1, backward + x]
                        + wide_ref[2, forward + x] * wide_ref[3, backward + x]
                    )
                    total = term if total is None else total + term
                sum_ref[block * size_y : (block + 1) * size_y, :] = total
            pooled_y = None
            for step in range(4):
                rows = sum_ref[pl.ds(step, blocks_x * blocks_y, stride=4), :]
                pooled_y = rows if pooled_y is None else pooled_y + rows
            pooled = split_dot(pooled_y, pool_z_ref[...], True)
            out_ref[index] = (pooled * (1.0 / 64.0)).reshape(blocks_x, blocks_y, blocks_z)
            return carry

        lax.fori_loop(0, count, per_offset, 0, unroll=True)

    return pl.pallas_call(
        kernel,
        grid_spec=pltpu.PrefetchScalarGridSpec(
            num_scalar_prefetch=1,
            grid=(1,),
            in_specs=[pl.BlockSpec(memory_space=pl.ANY) for _ in pieces]
            + [pl.BlockSpec((size_z, blocks_z), lambda i, offsets_ref: (0, 0))],
            out_specs=pl.BlockSpec((count, blocks_x, blocks_y, blocks_z), lambda i, offsets_ref: (0, 0, 0, 0)),
            scratch_shapes=[
                pltpu.VMEM((fields, span_x, size_y, size_z), jnp.float32),
                pltpu.VMEM((blocks_x * size_y, size_z), jnp.float32),
                pltpu.SemaphoreType.DMA((len(pieces),)),
            ],
        ),
        out_shape=jax.ShapeDtypeStruct((count, blocks_x, blocks_y, blocks_z), jnp.float32),
    )(offsets, *[piece[0] for piece in pieces], pool_z)


def conv_apply(padded, conv_weight, conv_bias):
    channels, span_x, span_y, span_z = padded.shape
    size_x, size_y, size_z = (span_x - 2, span_y - 2, span_z - 2)
    patches = jnp.stack(
        [
            padded[:, step_x : step_x + size_x, step_y : step_y + size_y, step_z : step_z + size_z]
            for step_x in range(3)
            for step_y in range(3)
            for step_z in range(3)
        ],
        axis=1,
    )
    patches = patches.reshape(channels * 27, size_x * size_y * size_z)
    matrix = conv_weight.reshape(conv_weight.shape[0], channels * 27)
    result = jnp.dot(
        matrix, patches, precision=lax.Precision.HIGHEST, preferred_element_type=jnp.float32
    )
    result = result + conv_bias[:, None]
    return result.reshape(conv_weight.shape[0], size_x, size_y * size_z)


def group_sum_windows(coarse, axis):
    count = lax.axis_size(axis)
    rows = coarse.shape[2] // count
    rimmed = jnp.pad(coarse, ((0, 0), (0, 0), (1, 1), (0, 0)))
    windows = jnp.stack(
        [lax.slice_in_dim(rimmed, k, k + (count - 1) * rows + 1, stride=rows, axis=2) for k in range(rows + 2)]
    )
    windows = jnp.moveaxis(windows, 3, 0)
    shape = windows.shape[1:]
    received = lax.all_to_all(windows.reshape(count, -1), axis, 0, 0, tiled=True)
    return jnp.moveaxis(received.sum(axis=0).reshape(shape), 0, 2)


def local(
    source_prev,
    source_now,
    receiver_prev,
    receiver_now,
    courant,
    source_cells,
    wavelet,
    receiver_cells,
    receiver_data,
    offsets,
    conv_weight,
    conv_bias,
):
    cells_x, size_y, size_z = courant.shape
    slab_index = lax.axis_index("gx")
    first_x = slab_index * cells_x
    previous = jnp.stack([source_prev[0], receiver_prev[0]])
    current = jnp.stack([source_now[0], receiver_now[0]])
    current_wide, previous_wide, courant_wide = input_halo(current, previous, courant, "gx")
    source_fields = inject(cells_x + 2, first_x - 1, source_cells[0], wavelet[0], size_y, size_z)
    receiver_fields = inject(cells_x + 2, first_x - 1, receiver_cells[0], receiver_data[0], size_y, size_z)
    levels = []
    for step_index in range(2):
        sources = jnp.stack([source_fields[step_index], receiver_fields[step_index]])
        if step_index == 0:
            step_previous, step_extended, step_courant = previous_wide, current_wide, courant_wide
        else:
            sources = sources[:, 1:-1]
            step_previous, step_extended, step_courant = current, levels[0], courant
        advanced = laplace_step(step_previous, step_extended, step_courant, sources)
        levels.append(advanced)
    levels_full = list(levels)
    levels[0] = levels[0][:, 1:-1]
    fields = jnp.concatenate(levels, axis=0)
    width = HMAX + 4
    low, high = halo_pieces(fields, "gx", width)
    pieces = [
        (low, 0, 0, 0, width),
        (levels_full[0], 0, width, 1, cells_x),
        (levels_full[1], 2, width, 0, cells_x),
        (high, 0, width + cells_x, 0, width),
    ]
    coarse = offset_image(pieces, offsets, HMAX, cells_x + 8)
    summed = group_sum_windows(coarse, "shot")
    window = jnp.pad(summed, ((0, 0), (0, 0), (0, 0), (1, 1)))
    return conv_apply(window, conv_weight, conv_bias)


def solution(mesh):
    in_specs = (
        P("shot", "gx", None, None),
        P("shot", "gx", None, None),
        P("shot", "gx", None, None),
        P("shot", "gx", None, None),
        P("gx", None, None),
        P("shot", None),
        P("shot", None, None),
        P("shot", None),
        P("shot", None, None),
        P(),
        P(),
        P(),
    )
    out_specs = P(None, "gx", "shot")
    return jax.shard_map(local, mesh=mesh, in_specs=in_specs, out_specs=out_specs, check_vma=False)
```

```python
import jax
import jax.numpy as jnp
from jax import lax
from jax.experimental import pallas as pl
from jax.experimental.pallas import tpu as pltpu
from jax.sharding import PartitionSpec as P

HMAX = 8


def padded_2(block, sides, width):
    for axis, dim in sides:
        count = lax.axis_size(axis)
        forward = [(i, i + 1) for i in range(count - 1)]
        backward = [(target, source) for source, target in forward]
        low = lax.ppermute(
            lax.slice_in_dim(block, block.shape[dim] - width, None, axis=dim), axis, forward
        )
        high = lax.ppermute(lax.slice_in_dim(block, 0, width, axis=dim), axis, backward)
        block = jnp.concatenate([low, block, high], axis=dim)
    return block


def halo_pieces(block, axis, width):
    count = lax.axis_size(axis)
    forward = [(i, i + 1) for i in range(count - 1)]
    backward = [(target, source) for source, target in forward]
    low = lax.ppermute(block[:, block.shape[1] - width :], axis, forward)
    high = lax.ppermute(block[:, :width], axis, backward)
    return low, high


def input_halo(current, previous, courant, axis):
    count = lax.axis_size(axis)
    forward = [(i, i + 1) for i in range(count - 1)]
    backward = [(target, source) for source, target in forward]
    fields, cells_x, size_y, size_z = current.shape

    def pack(now_planes, prev_planes, courant_planes):
        return jnp.concatenate(
            [now_planes.reshape(-1, size_y, size_z), prev_planes.reshape(-1, size_y, size_z), courant_planes]
        )

    def unpack(planes):
        now_planes = planes[: 2 * fields].reshape(fields, 2, size_y, size_z)
        prev_planes = planes[2 * fields : 3 * fields].reshape(fields, 1, size_y, size_z)
        return now_planes, prev_planes, planes[3 * fields :]

    low = lax.ppermute(
        pack(current[:, -2:], previous[:, -1:], courant[-1:]), axis, forward
    )
    high = lax.ppermute(pack(current[:, :2], previous[:, :1], courant[:1]), axis, backward)
    low_now, low_prev, low_courant = unpack(low)
    high_now, high_prev, high_courant = unpack(high)
    current_wide = jnp.concatenate([low_now, current, high_now], axis=1)
    previous_wide = jnp.concatenate([low_prev, previous, high_prev], axis=1)
    courant_wide = jnp.concatenate([low_courant, courant, high_courant], axis=0)
    return current_wide, previous_wide, courant_wide


def bf16_parts(value):
    high = value.astype(jnp.bfloat16)
    rest = value - high.astype(jnp.float32)
    middle = rest.astype(jnp.bfloat16)
    low = (rest - middle.astype(jnp.float32)).astype(jnp.bfloat16)
    return (high, middle, low)


def rounded_parts(value):
    high = lax.reduce_precision(value, exponent_bits=8, mantissa_bits=7)
    rest = value - high
    middle = lax.reduce_precision(rest, exponent_bits=8, mantissa_bits=7)
    low = rest - middle
    return (high.astype(jnp.bfloat16), middle.astype(jnp.bfloat16), low.astype(jnp.bfloat16))


def inject(cells_here, first_x, cell_index, amplitudes, size_y, size_z):
    plane_size = size_y * size_z
    column = cell_index // plane_size
    within = cell_index % plane_size
    row = (column - first_x) * size_y + within // size_z
    rows = (jnp.arange(cells_here * size_y)[:, None] == row[None, :]).astype(jnp.bfloat16)
    at_z = jnp.arange(size_z)[None, :] == (within % size_z)[:, None]
    fields = []
    for amplitude in amplitudes:
        placed = jnp.where(at_z, amplitude[:, None], 0.0)
        parts = jnp.concatenate(rounded_parts(placed), axis=1)
        sums = jnp.dot(rows, parts, preferred_element_type=jnp.float32)
        total = sums[:, :size_z] + sums[:, size_z : 2 * size_z] + sums[:, 2 * size_z :]
        fields.append(total.reshape(cells_here, size_y, size_z))
    return fields


def laplace_step(previous, extended, courant, sources):
    center = extended[:, 1:-1]
    padded = jnp.pad(center, ((0, 0), (0, 0), (1, 1), (1, 1)))
    laplace = extended[:, 2:] + extended[:, :-2]
    laplace = laplace + padded[:, :, 2:, 1:-1] + padded[:, :, :-2, 1:-1]
    laplace = laplace + padded[:, :, 1:-1, 2:] + padded[:, :, 1:-1, :-2] - 6.0 * center
    return 2.0 * center - previous + courant * laplace + sources


def pooling(size, group):
    fine = jnp.arange(size)[:, None] // group
    coarse = jnp.arange(size // group)[None, :]
    return (fine == coarse).astype(jnp.float32)


def split_dot(left, right, split_left):
    total = None
    if split_left:
        pieces = [(piece, right.astype(jnp.bfloat16)) for piece in bf16_parts(left)]
    else:
        pieces = [(left.astype(jnp.bfloat16), piece) for piece in bf16_parts(right)]
    for a, b in pieces:
        term = jnp.dot(a, b, preferred_element_type=jnp.float32)
        total = term if total is None else total + term
    return total


def offset_image(pieces, offsets, margin, cells_x):
    size_y, size_z = pieces[0][0].shape[2:]
    fields = max(first + array.shape[0] for array, first, _, _, _ in pieces)
    span_x = max(at + span for _, _, at, _, span in pieces)
    count = offsets.shape[0]
    blocks_x, blocks_y, blocks_z = cells_x // 4, size_y // 4, size_z // 4
    pool_z = pooling(size_z, 4)

    def kernel(offsets_ref, *refs):
        piece_refs = refs[: len(pieces)]
        pool_z_ref, out_ref, wide_ref, sum_ref, semaphores = refs[len(pieces) :]
        copies = []
        for k, (piece_ref, (array, first, at, taken, span)) in enumerate(zip(piece_refs, pieces)):
            source = piece_ref.at[:, taken : taken + span] if span != array.shape[1] else piece_ref
            target = wide_ref.at[first : first + array.shape[0], at : at + span]
            copies.append(pltpu.make_async_copy(source, target, semaphores.at[k]))
        for copy in copies:
            copy.start()
        for copy in copies:
            copy.wait()

        def per_offset(index, carry):
            offset_value = offsets_ref[index]
            forward = margin + offset_value
            backward = margin - offset_value
            for block in range(blocks_x):
                total = None
                for step in range(4):
                    x = block * 4 + step
                    term = (
                        wide_ref[0, forward + x] * wide_ref[1, backward + x]
                        + wide_ref[2, forward + x] * wide_ref[3, backward + x]
                    )
                    total = term if total is None else total + term
                sum_ref[block * size_y : (block + 1) * size_y, :] = total
            pooled_y = None
            for step in range(4):
                rows = sum_ref[pl.ds(step, blocks_x * blocks_y, stride=4), :]
                pooled_y = rows if pooled_y is None else pooled_y + rows
            pooled = split_dot(pooled_y, pool_z_ref[...], True)
            out_ref[index] = (pooled * (1.0 / 64.0)).reshape(blocks_x, blocks_y, blocks_z)
            return carry

        lax.fori_loop(0, count, per_offset, 0, unroll=True)

    return pl.pallas_call(
        kernel,
        grid_spec=pltpu.PrefetchScalarGridSpec(
            num_scalar_prefetch=1,
            grid=(1,),
            in_specs=[pl.BlockSpec(memory_space=pl.ANY) for _ in pieces]
            + [pl.BlockSpec((size_z, blocks_z), lambda i, offsets_ref: (0, 0))],
            out_specs=pl.BlockSpec((count, blocks_x, blocks_y, blocks_z), lambda i, offsets_ref: (0, 0, 0, 0)),
            scratch_shapes=[
                pltpu.VMEM((fields, span_x, size_y, size_z), jnp.float32),
                pltpu.VMEM((blocks_x * size_y, size_z), jnp.float32),
                pltpu.SemaphoreType.DMA((len(pieces),)),
            ],
        ),
        out_shape=jax.ShapeDtypeStruct((count, blocks_x, blocks_y, blocks_z), jnp.float32),
    )(offsets, *[piece[0] for piece in pieces], pool_z)


def conv_apply(padded, conv_weight, conv_bias):
    channels, span_x, span_y, span_z = padded.shape
    size_x, size_y, size_z = (span_x - 2, span_y - 2, span_z - 2)
    patches = jnp.stack(
        [
            padded[:, step_x : step_x + size_x, step_y : step_y + size_y, step_z : step_z + size_z]
            for step_x in range(3)
            for step_y in range(3)
            for step_z in range(3)
        ],
        axis=1,
    )
    patches = patches.reshape(channels * 27, size_x * size_y * size_z)
    matrix = conv_weight.reshape(conv_weight.shape[0], channels * 27)
    result = jnp.dot(
        matrix, patches, precision=lax.Precision.HIGHEST, preferred_element_type=jnp.float32
    )
    result = result + conv_bias[:, None]
    return result.reshape(conv_weight.shape[0], size_x, size_y * size_z)


def group_sum_windows(coarse, axis):
    count = lax.axis_size(axis)
    rows = coarse.shape[2] // count
    rimmed = jnp.pad(coarse, ((0, 0), (0, 0), (1, 1), (0, 0)))
    windows = jnp.stack(
        [lax.slice_in_dim(rimmed, k, k + (count - 1) * rows + 1, stride=rows, axis=2) for k in range(rows + 2)]
    )
    windows = jnp.moveaxis(windows, 3, 0)
    shape = windows.shape[1:]
    received = lax.all_to_all(windows.reshape(count, -1), axis, 0, 0, tiled=True)
    return jnp.moveaxis(received.sum(axis=0).reshape(shape), 0, 2)


def local(
    source_prev,
    source_now,
    receiver_prev,
    receiver_now,
    courant,
    source_cells,
    wavelet,
    receiver_cells,
    receiver_data,
    offsets,
    conv_weight,
    conv_bias,
):
    cells_x, size_y, size_z = courant.shape
    slab_index = lax.axis_index("gx")
    first_x = slab_index * cells_x
    previous = jnp.stack([source_prev[0], receiver_prev[0]])
    current = jnp.stack([source_now[0], receiver_now[0]])
    current_wide, previous_wide, courant_wide = input_halo(current, previous, courant, "gx")
    source_fields = inject(cells_x + 2, first_x - 1, source_cells[0], wavelet[0], size_y, size_z)
    receiver_fields = inject(cells_x + 2, first_x - 1, receiver_cells[0], receiver_data[0], size_y, size_z)
    levels = []
    for step_index in range(2):
        sources = jnp.stack([source_fields[step_index], receiver_fields[step_index]])
        if step_index == 0:
            step_previous, step_extended, step_courant = previous_wide, current_wide, courant_wide
        else:
            sources = sources[:, 1:-1]
            step_previous, step_extended, step_courant = current, levels[0], courant
        advanced = laplace_step(step_previous, step_extended, step_courant, sources)
        levels.append(advanced)
    levels_full = list(levels)
    levels[0] = levels[0][:, 1:-1]
    fields = jnp.concatenate(levels, axis=0)
    width = HMAX
    low, high = halo_pieces(fields, "gx", width)
    pieces = [
        (low, 0, 0, 0, width),
        (levels_full[0], 0, width, 1, cells_x),
        (levels_full[1], 2, width, 0, cells_x),
        (high, 0, width + cells_x, 0, width),
    ]
    coarse = offset_image(pieces, offsets, HMAX, cells_x)
    summed = group_sum_windows(coarse, "shot")
    rimmed = padded_2(summed, (("gx", 1),), 1)
    window = jnp.pad(rimmed, ((0, 0), (0, 0), (0, 0), (1, 1)))
    return conv_apply(window, conv_weight, conv_bias)


def solution(mesh):
    in_specs = (
        P("shot", "gx", None, None),
        P("shot", "gx", None, None),
        P("shot", "gx", None, None),
        P("shot", "gx", None, None),
        P("gx", None, None),
        P("shot", None),
        P("shot", None, None),
        P("shot", None),
        P("shot", None, None),
        P(),
        P(),
        P(),
    )
    out_specs = P(None, "gx", "shot")
    return jax.shard_map(local, mesh=mesh, in_specs=in_specs, out_specs=out_specs, check_vma=False)
```

```python
import jax
import jax.numpy as jnp
from jax import lax
from jax.experimental import pallas as pl
from jax.experimental.pallas import tpu as pltpu
from jax.sharding import PartitionSpec as P

HMAX = 8


def padded_2(block, sides, width):
    for axis, dim in sides:
        count = lax.axis_size(axis)
        forward = [(i, i + 1) for i in range(count - 1)]
        backward = [(target, source) for source, target in forward]
        low = lax.ppermute(
            lax.slice_in_dim(block, block.shape[dim] - width, None, axis=dim), axis, forward
        )
        high = lax.ppermute(lax.slice_in_dim(block, 0, width, axis=dim), axis, backward)
        block = jnp.concatenate([low, block, high], axis=dim)
    return block


def halo_pieces(block, axis, width):
    count = lax.axis_size(axis)
    forward = [(i, i + 1) for i in range(count - 1)]
    backward = [(target, source) for source, target in forward]
    low = lax.ppermute(block[:, block.shape[1] - width :], axis, forward)
    high = lax.ppermute(block[:, :width], axis, backward)
    return low, high


def input_halo(current, previous, courant, axis):
    count = lax.axis_size(axis)
    forward = [(i, i + 1) for i in range(count - 1)]
    backward = [(target, source) for source, target in forward]
    fields, cells_x, size_y, size_z = current.shape

    def pack(now_planes, prev_planes, courant_planes):
        return jnp.concatenate(
            [now_planes.reshape(-1, size_y, size_z), prev_planes.reshape(-1, size_y, size_z), courant_planes]
        )

    def unpack(planes):
        now_planes = planes[: 2 * fields].reshape(fields, 2, size_y, size_z)
        prev_planes = planes[2 * fields : 3 * fields].reshape(fields, 1, size_y, size_z)
        return now_planes, prev_planes, planes[3 * fields :]

    low = lax.ppermute(
        pack(current[:, -2:], previous[:, -1:], courant[-1:]), axis, forward
    )
    high = lax.ppermute(pack(current[:, :2], previous[:, :1], courant[:1]), axis, backward)
    low_now, low_prev, low_courant = unpack(low)
    high_now, high_prev, high_courant = unpack(high)
    current_wide = jnp.concatenate([low_now, current, high_now], axis=1)
    previous_wide = jnp.concatenate([low_prev, previous, high_prev], axis=1)
    courant_wide = jnp.concatenate([low_courant, courant, high_courant], axis=0)
    return current_wide, previous_wide, courant_wide


def bf16_parts(value):
    high = value.astype(jnp.bfloat16)
    rest = value - high.astype(jnp.float32)
    middle = rest.astype(jnp.bfloat16)
    low = (rest - middle.astype(jnp.float32)).astype(jnp.bfloat16)
    return (high, middle, low)


def rounded_parts(value):
    high = lax.reduce_precision(value, exponent_bits=8, mantissa_bits=7)
    rest = value - high
    middle = lax.reduce_precision(rest, exponent_bits=8, mantissa_bits=7)
    low = rest - middle
    return (high.astype(jnp.bfloat16), middle.astype(jnp.bfloat16), low.astype(jnp.bfloat16))


def inject(cells_here, first_x, cell_index, amplitudes, size_y, size_z):
    plane_size = size_y * size_z
    column = cell_index // plane_size
    within = cell_index % plane_size
    row = (column - first_x) * size_y + within // size_z
    rows = (jnp.arange(cells_here * size_y)[:, None] == row[None, :]).astype(jnp.bfloat16)
    at_z = jnp.arange(size_z)[None, :] == (within % size_z)[:, None]
    fields = []
    for amplitude in amplitudes:
        placed = jnp.where(at_z, amplitude[:, None], 0.0)
        parts = jnp.concatenate(rounded_parts(placed), axis=1)
        sums = jnp.dot(rows, parts, preferred_element_type=jnp.float32)
        total = sums[:, :size_z] + sums[:, size_z : 2 * size_z] + sums[:, 2 * size_z :]
        fields.append(total.reshape(cells_here, size_y, size_z))
    return fields


def laplace_step(previous, extended, courant, sources):
    center = extended[:, 1:-1]
    padded = jnp.pad(center, ((0, 0), (0, 0), (1, 1), (1, 1)))
    laplace = extended[:, 2:] + extended[:, :-2]
    laplace = laplace + padded[:, :, 2:, 1:-1] + padded[:, :, :-2, 1:-1]
    laplace = laplace + padded[:, :, 1:-1, 2:] + padded[:, :, 1:-1, :-2] - 6.0 * center
    return 2.0 * center - previous + courant * laplace + sources


def pooling(size, group):
    fine = jnp.arange(size)[:, None] // group
    coarse = jnp.arange(size // group)[None, :]
    return (fine == coarse).astype(jnp.float32)


def split_dot(left, right, split_left):
    total = None
    if split_left:
        pieces = [(piece, right.astype(jnp.bfloat16)) for piece in bf16_parts(left)]
    else:
        pieces = [(left.astype(jnp.bfloat16), piece) for piece in bf16_parts(right)]
    for a, b in pieces:
        term = jnp.dot(a, b, preferred_element_type=jnp.float32)
        total = term if total is None else total + term
    return total


def offset_image(pieces, offsets, margin, cells_x):
    size_y, size_z = pieces[0][0].shape[2:]
    fields = max(first + array.shape[0] for array, first, _, _, _ in pieces)
    span_x = max(at + span for _, _, at, _, span in pieces)
    count = offsets.shape[0]
    blocks_x, blocks_y, blocks_z = cells_x // 4, size_y // 4, size_z // 4
    pool_z = pooling(size_z, 4)

    def kernel(offsets_ref, *refs):
        piece_refs = refs[: len(pieces)]
        pool_z_ref, out_ref, wide_ref, sum_ref, semaphores = refs[len(pieces) :]
        copies = []
        for k, (piece_ref, (array, first, at, taken, span)) in enumerate(zip(piece_refs, pieces)):
            source = piece_ref.at[:, taken : taken + span] if span != array.shape[1] else piece_ref
            target = wide_ref.at[first : first + array.shape[0], at : at + span]
            copies.append(pltpu.make_async_copy(source, target, semaphores.at[k]))
        for copy in copies:
            copy.start()
        for copy in copies:
            copy.wait()

        def per_offset(index, carry):
            offset_value = offsets_ref[index]
            forward = margin + offset_value
            backward = margin - offset_value
            for block in range(blocks_x):
                total = None
                for step in range(4):
                    x = block * 4 + step
                    term = (
                        wide_ref[0, forward + x] * wide_ref[1, backward + x]
                        + wide_ref[2, forward + x] * wide_ref[3, backward + x]
                    )
                    total = term if total is None else total + term
                sum_ref[block * size_y : (block + 1) * size_y, :] = total
            pooled_y = None
            for step in range(4):
                rows = sum_ref[pl.ds(step, blocks_x * blocks_y, stride=4), :]
                pooled_y = rows if pooled_y is None else pooled_y + rows
            pooled = split_dot(pooled_y, pool_z_ref[...], True)
            out_ref[index] = (pooled * (1.0 / 64.0)).reshape(blocks_x, blocks_y, blocks_z)
            return carry

        lax.fori_loop(0, count, per_offset, 0, unroll=True)

    return pl.pallas_call(
        kernel,
        grid_spec=pltpu.PrefetchScalarGridSpec(
            num_scalar_prefetch=1,
            grid=(1,),
            in_specs=[pl.BlockSpec(memory_space=pl.ANY) for _ in pieces]
            + [pl.BlockSpec((size_z, blocks_z), lambda i, offsets_ref: (0, 0))],
            out_specs=pl.BlockSpec((count, blocks_x, blocks_y, blocks_z), lambda i, offsets_ref: (0, 0, 0, 0)),
            scratch_shapes=[
                pltpu.VMEM((fields, span_x, size_y, size_z), jnp.float32),
                pltpu.VMEM((blocks_x * size_y, size_z), jnp.float32),
                pltpu.SemaphoreType.DMA((len(pieces),)),
            ],
        ),
        out_shape=jax.ShapeDtypeStruct((count, blocks_x, blocks_y, blocks_z), jnp.float32),
    )(offsets, *[piece[0] for piece in pieces], pool_z)


def conv_apply(window, conv_weight, conv_bias):
    result = lax.conv_general_dilated(
        window[None],
        conv_weight,
        window_strides=(1, 1, 1),
        padding=((0, 0), (0, 0), (1, 1)),
        dimension_numbers=("NCDHW", "OIDHW", "NCDHW"),
        precision=lax.Precision.HIGHEST,
        preferred_element_type=jnp.float32,
    )[0]
    result = result + conv_bias[:, None, None, None]
    return result.reshape(conv_weight.shape[0], result.shape[1], result.shape[2] * result.shape[3])


def group_sum_windows(coarse, axis):
    count = lax.axis_size(axis)
    rows = coarse.shape[2] // count
    rimmed = jnp.pad(coarse, ((0, 0), (0, 0), (1, 1), (0, 0)))
    windows = jnp.stack(
        [lax.slice_in_dim(rimmed, k, k + (count - 1) * rows + 1, stride=rows, axis=2) for k in range(rows + 2)]
    )
    windows = jnp.moveaxis(windows, 3, 0)
    shape = windows.shape[1:]
    received = lax.all_to_all(windows.reshape(count, -1), axis, 0, 0, tiled=True)
    return jnp.moveaxis(received.sum(axis=0).reshape(shape), 0, 2)


def local(
    source_prev,
    source_now,
    receiver_prev,
    receiver_now,
    courant,
    source_cells,
    wavelet,
    receiver_cells,
    receiver_data,
    offsets,
    conv_weight,
    conv_bias,
):
    cells_x, size_y, size_z = courant.shape
    slab_index = lax.axis_index("gx")
    first_x = slab_index * cells_x
    previous = jnp.stack([source_prev[0], receiver_prev[0]])
    current = jnp.stack([source_now[0], receiver_now[0]])
    current_wide, previous_wide, courant_wide = input_halo(current, previous, courant, "gx")
    source_fields = inject(cells_x + 2, first_x - 1, source_cells[0], wavelet[0], size_y, size_z)
    receiver_fields = inject(cells_x + 2, first_x - 1, receiver_cells[0], receiver_data[0], size_y, size_z)
    levels = []
    for step_index in range(2):
        sources = jnp.stack([source_fields[step_index], receiver_fields[step_index]])
        if step_index == 0:
            step_previous, step_extended, step_courant = previous_wide, current_wide, courant_wide
        else:
            sources = sources[:, 1:-1]
            step_previous, step_extended, step_courant = current, levels[0], courant
        advanced = laplace_step(step_previous, step_extended, step_courant, sources)
        levels.append(advanced)
    levels_full = list(levels)
    levels[0] = levels[0][:, 1:-1]
    fields = jnp.concatenate(levels, axis=0)
    width = HMAX + 4
    low, high = halo_pieces(fields, "gx", width)
    pieces = [
        (low, 0, 0, 0, width),
        (levels_full[0], 0, width, 1, cells_x),
        (levels_full[1], 2, width, 0, cells_x),
        (high, 0, width + cells_x, 0, width),
    ]
    coarse = offset_image(pieces, offsets, HMAX, cells_x + 8)
    summed = group_sum_windows(coarse, "shot")
    return conv_apply(summed, conv_weight, conv_bias)


def solution(mesh):
    in_specs = (
        P("shot", "gx", None, None),
        P("shot", "gx", None, None),
        P("shot", "gx", None, None),
        P("shot", "gx", None, None),
        P("gx", None, None),
        P("shot", None),
        P("shot", None, None),
        P("shot", None),
        P("shot", None, None),
        P(),
        P(),
        P(),
    )
    out_specs = P(None, "gx", "shot")
    return jax.shard_map(local, mesh=mesh, in_specs=in_specs, out_specs=out_specs, check_vma=False)
```

```python
import jax
import jax.numpy as jnp
from jax import lax
from jax.experimental import pallas as pl
from jax.experimental.pallas import tpu as pltpu
from jax.sharding import PartitionSpec as P

HMAX = 8


def padded_2(block, sides, width):
    for axis, dim in sides:
        count = lax.axis_size(axis)
        forward = [(i, i + 1) for i in range(count - 1)]
        backward = [(target, source) for source, target in forward]
        low = lax.ppermute(
            lax.slice_in_dim(block, block.shape[dim] - width, None, axis=dim), axis, forward
        )
        high = lax.ppermute(lax.slice_in_dim(block, 0, width, axis=dim), axis, backward)
        block = jnp.concatenate([low, block, high], axis=dim)
    return block


def halo_pieces(block, axis, width):
    count = lax.axis_size(axis)
    forward = [(i, i + 1) for i in range(count - 1)]
    backward = [(target, source) for source, target in forward]
    low = lax.ppermute(block[:, block.shape[1] - width :], axis, forward)
    high = lax.ppermute(block[:, :width], axis, backward)
    return low, high


def input_halo(current, previous, courant, axis):
    count = lax.axis_size(axis)
    forward = [(i, i + 1) for i in range(count - 1)]
    backward = [(target, source) for source, target in forward]
    fields, cells_x, size_y, size_z = current.shape

    def pack(now_planes, prev_planes, courant_planes):
        return jnp.concatenate(
            [now_planes.reshape(-1, size_y, size_z), prev_planes.reshape(-1, size_y, size_z), courant_planes]
        )

    def unpack(planes):
        now_planes = planes[: 2 * fields].reshape(fields, 2, size_y, size_z)
        prev_planes = planes[2 * fields : 3 * fields].reshape(fields, 1, size_y, size_z)
        return now_planes, prev_planes, planes[3 * fields :]

    low = lax.ppermute(
        pack(current[:, -2:], previous[:, -1:], courant[-1:]), axis, forward
    )
    high = lax.ppermute(pack(current[:, :2], previous[:, :1], courant[:1]), axis, backward)
    low_now, low_prev, low_courant = unpack(low)
    high_now, high_prev, high_courant = unpack(high)
    current_wide = jnp.concatenate([low_now, current, high_now], axis=1)
    previous_wide = jnp.concatenate([low_prev, previous, high_prev], axis=1)
    courant_wide = jnp.concatenate([low_courant, courant, high_courant], axis=0)
    return current_wide, previous_wide, courant_wide


def bf16_parts(value):
    high = value.astype(jnp.bfloat16)
    rest = value - high.astype(jnp.float32)
    middle = rest.astype(jnp.bfloat16)
    low = (rest - middle.astype(jnp.float32)).astype(jnp.bfloat16)
    return (high, middle, low)


def rounded_parts(value):
    high = lax.reduce_precision(value, exponent_bits=8, mantissa_bits=7)
    rest = value - high
    middle = lax.reduce_precision(rest, exponent_bits=8, mantissa_bits=7)
    low = rest - middle
    return (high.astype(jnp.bfloat16), middle.astype(jnp.bfloat16), low.astype(jnp.bfloat16))


def inject(cells_here, first_x, cell_index, amplitudes, size_y, size_z):
    plane_size = size_y * size_z
    column = cell_index // plane_size
    within = cell_index % plane_size
    row = (column - first_x) * size_y + within // size_z
    rows = (jnp.arange(cells_here * size_y)[:, None] == row[None, :]).astype(jnp.bfloat16)
    at_z = jnp.arange(size_z)[None, :] == (within % size_z)[:, None]
    fields = []
    for amplitude in amplitudes:
        placed = jnp.where(at_z, amplitude[:, None], 0.0)
        parts = jnp.concatenate(rounded_parts(placed), axis=1)
        sums = jnp.dot(rows, parts, preferred_element_type=jnp.float32)
        total = sums[:, :size_z] + sums[:, size_z : 2 * size_z] + sums[:, 2 * size_z :]
        fields.append(total.reshape(cells_here, size_y, size_z))
    return fields


def laplace_step(previous, extended, courant, sources):
    center = extended[:, 1:-1]
    padded = jnp.pad(center, ((0, 0), (0, 0), (1, 1), (1, 1)))
    laplace = extended[:, 2:] + extended[:, :-2]
    laplace = laplace + padded[:, :, 2:, 1:-1] + padded[:, :, :-2, 1:-1]
    laplace = laplace + padded[:, :, 1:-1, 2:] + padded[:, :, 1:-1, :-2] - 6.0 * center
    return 2.0 * center - previous + courant * laplace + sources


def pooling(size, group):
    fine = jnp.arange(size)[:, None] // group
    coarse = jnp.arange(size // group)[None, :]
    return (fine == coarse).astype(jnp.float32)


def split_dot(left, right, split_left):
    total = None
    if split_left:
        pieces = [(piece, right.astype(jnp.bfloat16)) for piece in bf16_parts(left)]
    else:
        pieces = [(left.astype(jnp.bfloat16), piece) for piece in bf16_parts(right)]
    for a, b in pieces:
        term = jnp.dot(a, b, preferred_element_type=jnp.float32)
        total = term if total is None else total + term
    return total


def offset_image(pieces, offsets, margin, cells_x):
    size_y, size_z = pieces[0][0].shape[2:]
    fields = max(first + array.shape[0] for array, first, _, _, _ in pieces)
    span_x = max(at + span for _, _, at, _, span in pieces)
    count = offsets.shape[0]
    blocks_x, blocks_y, blocks_z = cells_x // 4, size_y // 4, size_z // 4
    pool_z = pooling(size_z, 4)

    def kernel(offsets_ref, *refs):
        piece_refs = refs[: len(pieces)]
        pool_z_ref, out_ref, wide_ref, sum_ref, semaphores = refs[len(pieces) :]
        copies = []
        for k, (piece_ref, (array, first, at, taken, span)) in enumerate(zip(piece_refs, pieces)):
            source = piece_ref.at[:, taken : taken + span] if span != array.shape[1] else piece_ref
            target = wide_ref.at[first : first + array.shape[0], at : at + span]
            copies.append(pltpu.make_async_copy(source, target, semaphores.at[k]))
        for copy in copies:
            copy.start()
        for copy in copies:
            copy.wait()

        def per_offset(index, carry):
            offset_value = offsets_ref[index]
            forward = margin + offset_value
            backward = margin - offset_value
            for block in range(blocks_x):
                total = None
                for step in range(4):
                    x = block * 4 + step
                    term = (
                        wide_ref[0, forward + x] * wide_ref[1, backward + x]
                        + wide_ref[2, forward + x] * wide_ref[3, backward + x]
                    )
                    total = term if total is None else total + term
                sum_ref[block * size_y : (block + 1) * size_y, :] = total
            pooled_y = None
            for step in range(4):
                rows = sum_ref[pl.ds(step, blocks_x * blocks_y, stride=4), :]
                pooled_y = rows if pooled_y is None else pooled_y + rows
            pooled = split_dot(pooled_y, pool_z_ref[...], True)
            out_ref[index] = (pooled * (1.0 / 64.0)).reshape(blocks_x, blocks_y, blocks_z)
            return carry

        lax.fori_loop(0, count, per_offset, 0, unroll=True)

    return pl.pallas_call(
        kernel,
        grid_spec=pltpu.PrefetchScalarGridSpec(
            num_scalar_prefetch=1,
            grid=(1,),
            in_specs=[pl.BlockSpec(memory_space=pl.ANY) for _ in pieces]
            + [pl.BlockSpec((size_z, blocks_z), lambda i, offsets_ref: (0, 0))],
            out_specs=pl.BlockSpec((count, blocks_x, blocks_y, blocks_z), lambda i, offsets_ref: (0, 0, 0, 0)),
            scratch_shapes=[
                pltpu.VMEM((fields, span_x, size_y, size_z), jnp.float32),
                pltpu.VMEM((blocks_x * size_y, size_z), jnp.float32),
                pltpu.SemaphoreType.DMA((len(pieces),)),
            ],
        ),
        out_shape=jax.ShapeDtypeStruct((count, blocks_x, blocks_y, blocks_z), jnp.float32),
    )(offsets, *[piece[0] for piece in pieces], pool_z)


def conv_apply(padded, conv_weight, conv_bias):
    channels, span_x, span_y, span_z = padded.shape
    size_x, size_y, size_z = (span_x - 2, span_y - 2, span_z - 2)
    patches = jnp.stack(
        [
            padded[:, step_x : step_x + size_x, step_y : step_y + size_y, step_z : step_z + size_z]
            for step_x in range(3)
            for step_y in range(3)
            for step_z in range(3)
        ],
        axis=1,
    )
    patches = patches.reshape(channels * 27, size_x * size_y * size_z)
    matrix = conv_weight.reshape(conv_weight.shape[0], channels * 27)
    result = jnp.dot(
        matrix, patches, precision=lax.Precision.HIGHEST, preferred_element_type=jnp.float32
    )
    result = result + conv_bias[:, None]
    return result.reshape(conv_weight.shape[0], size_x, size_y * size_z)


def group_sum_windows(coarse, axis):
    count = lax.axis_size(axis)
    rows = coarse.shape[2] // count
    rimmed = jnp.pad(coarse, ((0, 0), (0, 0), (1, 1), (0, 0)))
    windows = jnp.stack(
        [lax.slice_in_dim(rimmed, k, k + (count - 1) * rows + 1, stride=rows, axis=2) for k in range(rows + 2)]
    )
    windows = jnp.moveaxis(windows, 3, 0)
    shape = windows.shape[1:]
    received = lax.all_to_all(windows.reshape(count, -1), axis, 0, 0, tiled=True)
    return jnp.moveaxis(received.sum(axis=0).reshape(shape), 0, 2)


def local(
    source_prev,
    source_now,
    receiver_prev,
    receiver_now,
    courant,
    source_cells,
    wavelet,
    receiver_cells,
    receiver_data,
    offsets,
    conv_weight,
    conv_bias,
):
    cells_x, size_y, size_z = courant.shape
    slab_index = lax.axis_index("gx")
    first_x = slab_index * cells_x
    prev_list = [source_prev[0], receiver_prev[0]]
    now_list = [source_now[0], receiver_now[0]]
    count = lax.axis_size("gx")
    forward = [(i, i + 1) for i in range(count - 1)]
    backward = [(target, source) for source, target in forward]
    low = lax.ppermute(
        jnp.concatenate([now[-2:] for now in now_list] + [prev[-1:] for prev in prev_list] + [courant[-1:]]),
        "gx",
        forward,
    )
    high = lax.ppermute(
        jnp.concatenate([now[:2] for now in now_list] + [prev[:1] for prev in prev_list] + [courant[:1]]),
        "gx",
        backward,
    )
    fields = len(now_list)
    courant_wide = jnp.concatenate([low[3 * fields :], courant, high[3 * fields :]])
    injected = [
        inject(cells_x + 2, first_x - 1, source_cells[0], wavelet[0], size_y, size_z),
        inject(cells_x + 2, first_x - 1, receiver_cells[0], receiver_data[0], size_y, size_z),
    ]
    first_levels = []
    second_levels = []
    for field in range(fields):
        now_wide = jnp.concatenate(
            [low[2 * field : 2 * field + 2], now_list[field], high[2 * field : 2 * field + 2]]
        )
        prev_wide = jnp.concatenate(
            [
                low[2 * fields + field : 2 * fields + field + 1],
                prev_list[field],
                high[2 * fields + field : 2 * fields + field + 1],
            ]
        )
        first = laplace_step(prev_wide[None], now_wide[None], courant_wide, injected[field][0][None])
        second = laplace_step(now_list[field][None], first, courant, injected[field][1][None, 1:-1])
        first_levels.append(first)
        second_levels.append(second)
    width = HMAX + 4
    slab = jnp.concatenate([level[:, 1:-1] for level in first_levels] + second_levels)
    low_halo, high_halo = halo_pieces(slab, "gx", width)
    pieces = [(low_halo, 0, 0, 0, width)]
    pieces += [(level, field, width, 1, cells_x) for field, level in enumerate(first_levels)]
    pieces += [(level, fields + field, width, 0, cells_x) for field, level in enumerate(second_levels)]
    pieces += [(high_halo, 0, width + cells_x, 0, width)]
    coarse = offset_image(pieces, offsets, HMAX, cells_x + 8)
    summed = group_sum_windows(coarse, "shot")
    window = jnp.pad(summed, ((0, 0), (0, 0), (0, 0), (1, 1)))
    return conv_apply(window, conv_weight, conv_bias)


def solution(mesh):
    in_specs = (
        P("shot", "gx", None, None),
        P("shot", "gx", None, None),
        P("shot", "gx", None, None),
        P("shot", "gx", None, None),
        P("gx", None, None),
        P("shot", None),
        P("shot", None, None),
        P("shot", None),
        P("shot", None, None),
        P(),
        P(),
        P(),
    )
    out_specs = P(None, "gx", "shot")
    return jax.shard_map(local, mesh=mesh, in_specs=in_specs, out_specs=out_specs, check_vma=False)
```

```python
import jax
import jax.numpy as jnp
from jax import lax
from jax.experimental import pallas as pl
from jax.experimental.pallas import tpu as pltpu
from jax.sharding import PartitionSpec as P

HMAX = 8


def padded_2(block, sides, width):
    for axis, dim in sides:
        count = lax.axis_size(axis)
        forward = [(i, i + 1) for i in range(count - 1)]
        backward = [(target, source) for source, target in forward]
        low = lax.ppermute(
            lax.slice_in_dim(block, block.shape[dim] - width, None, axis=dim), axis, forward
        )
        high = lax.ppermute(lax.slice_in_dim(block, 0, width, axis=dim), axis, backward)
        block = jnp.concatenate([low, block, high], axis=dim)
    return block


def halo_pieces(block, axis, width):
    count = lax.axis_size(axis)
    forward = [(i, i + 1) for i in range(count - 1)]
    backward = [(target, source) for source, target in forward]
    low = lax.ppermute(block[:, block.shape[1] - width :], axis, forward)
    high = lax.ppermute(block[:, :width], axis, backward)
    return low, high


def input_halo(current, previous, courant, axis):
    count = lax.axis_size(axis)
    forward = [(i, i + 1) for i in range(count - 1)]
    backward = [(target, source) for source, target in forward]
    fields, cells_x, size_y, size_z = current.shape

    def pack(now_planes, prev_planes, courant_planes):
        return jnp.concatenate(
            [now_planes.reshape(-1, size_y, size_z), prev_planes.reshape(-1, size_y, size_z), courant_planes]
        )

    def unpack(planes):
        now_planes = planes[: 2 * fields].reshape(fields, 2, size_y, size_z)
        prev_planes = planes[2 * fields : 3 * fields].reshape(fields, 1, size_y, size_z)
        return now_planes, prev_planes, planes[3 * fields :]

    low = lax.ppermute(
        pack(current[:, -2:], previous[:, -1:], courant[-1:]), axis, forward
    )
    high = lax.ppermute(pack(current[:, :2], previous[:, :1], courant[:1]), axis, backward)
    low_now, low_prev, low_courant = unpack(low)
    high_now, high_prev, high_courant = unpack(high)
    current_wide = jnp.concatenate([low_now, current, high_now], axis=1)
    previous_wide = jnp.concatenate([low_prev, previous, high_prev], axis=1)
    courant_wide = jnp.concatenate([low_courant, courant, high_courant], axis=0)
    return current_wide, previous_wide, courant_wide


def bf16_parts(value):
    high = value.astype(jnp.bfloat16)
    rest = value - high.astype(jnp.float32)
    middle = rest.astype(jnp.bfloat16)
    low = (rest - middle.astype(jnp.float32)).astype(jnp.bfloat16)
    return (high, middle, low)


def rounded_parts(value):
    high = lax.reduce_precision(value, exponent_bits=8, mantissa_bits=7)
    rest = value - high
    middle = lax.reduce_precision(rest, exponent_bits=8, mantissa_bits=7)
    low = rest - middle
    return (high.astype(jnp.bfloat16), middle.astype(jnp.bfloat16), low.astype(jnp.bfloat16))


def inject(cells_here, first_x, cell_index, amplitudes, size_y, size_z):
    plane_size = size_y * size_z
    column = cell_index // plane_size
    within = cell_index % plane_size
    row = (column - first_x) * size_y + within // size_z
    rows = (jnp.arange(cells_here * size_y)[:, None] == row[None, :]).astype(jnp.bfloat16)
    at_z = jnp.arange(size_z)[None, :] == (within % size_z)[:, None]
    fields = []
    for amplitude in amplitudes:
        placed = jnp.where(at_z, amplitude[:, None], 0.0)
        parts = jnp.concatenate(rounded_parts(placed), axis=1)
        sums = jnp.dot(rows, parts, preferred_element_type=jnp.float32)
        total = sums[:, :size_z] + sums[:, size_z : 2 * size_z] + sums[:, 2 * size_z :]
        fields.append(total.reshape(cells_here, size_y, size_z))
    return fields


def laplace_step(previous, extended, courant, sources):
    center = extended[:, 1:-1]
    padded = jnp.pad(center, ((0, 0), (0, 0), (1, 1), (1, 1)))
    laplace = extended[:, 2:] + extended[:, :-2]
    laplace = laplace + padded[:, :, 2:, 1:-1] + padded[:, :, :-2, 1:-1]
    laplace = laplace + padded[:, :, 1:-1, 2:] + padded[:, :, 1:-1, :-2] - 6.0 * center
    return 2.0 * center - previous + courant * laplace + sources


def pooling(size, group):
    fine = jnp.arange(size)[:, None] // group
    coarse = jnp.arange(size // group)[None, :]
    return (fine == coarse).astype(jnp.float32)


def split_dot(left, right, split_left):
    total = None
    if split_left:
        pieces = [(piece, right.astype(jnp.bfloat16)) for piece in bf16_parts(left)]
    else:
        pieces = [(left.astype(jnp.bfloat16), piece) for piece in bf16_parts(right)]
    for a, b in pieces:
        term = jnp.dot(a, b, preferred_element_type=jnp.float32)
        total = term if total is None else total + term
    return total


def offset_image(pieces, offsets, margin, cells_x):
    size_y, size_z = pieces[0][0].shape[2:]
    fields = max(first + array.shape[0] for array, first, _, _, _ in pieces)
    span_x = max(at + span for _, _, at, _, span in pieces)
    count = offsets.shape[0]
    blocks_x, blocks_y, blocks_z = cells_x // 4, size_y // 4, size_z // 4
    pool_z = pooling(size_z, 4)

    def kernel(offsets_ref, *refs):
        piece_refs = refs[: len(pieces)]
        pool_z_ref, out_ref, wide_ref, sum_ref, semaphores = refs[len(pieces) :]
        copies = []
        for k, (piece_ref, (array, first, at, taken, span)) in enumerate(zip(piece_refs, pieces)):
            source = piece_ref.at[:, taken : taken + span] if span != array.shape[1] else piece_ref
            target = wide_ref.at[first : first + array.shape[0], at : at + span]
            copies.append(pltpu.make_async_copy(source, target, semaphores.at[k]))
        for copy in copies:
            copy.start()
        high_at = max(at for _, _, at, _, _ in pieces)
        early = [block for block in range(blocks_x) if 4 * block + 3 + 2 * margin <= high_at - 1]
        late = [block for block in range(blocks_x) if block not in early]
        waited = [copy for copy, piece in zip(copies, pieces) if piece[2] < high_at]
        for copy in waited:
            copy.wait()

        def products(block_list):
            for index in range(count):
                offset_value = offsets_ref[index]
                forward = margin + offset_value
                backward = margin - offset_value
                for block in block_list:
                    total = None
                    for step in range(4):
                        x = block * 4 + step
                        term = (
                            wide_ref[0, forward + x] * wide_ref[1, backward + x]
                            + wide_ref[2, forward + x] * wide_ref[3, backward + x]
                        )
                        total = term if total is None else total + term
                    sum_ref[index, block * size_y : (block + 1) * size_y, :] = total

        products(early)
        for copy, piece in zip(copies, pieces):
            if piece[2] >= high_at:
                copy.wait()
        products(late)
        for index in range(count):
            pooled_y = None
            for step in range(4):
                rows = sum_ref.at[index][pl.ds(step, blocks_x * blocks_y, stride=4), :]
                pooled_y = rows if pooled_y is None else pooled_y + rows
            pooled = split_dot(pooled_y, pool_z_ref[...], True)
            out_ref[index] = (pooled * (1.0 / 64.0)).reshape(blocks_x, blocks_y, blocks_z)

    return pl.pallas_call(
        kernel,
        grid_spec=pltpu.PrefetchScalarGridSpec(
            num_scalar_prefetch=1,
            grid=(1,),
            in_specs=[pl.BlockSpec(memory_space=pl.ANY) for _ in pieces]
            + [pl.BlockSpec((size_z, blocks_z), lambda i, offsets_ref: (0, 0))],
            out_specs=pl.BlockSpec((count, blocks_x, blocks_y, blocks_z), lambda i, offsets_ref: (0, 0, 0, 0)),
            scratch_shapes=[
                pltpu.VMEM((fields, span_x, size_y, size_z), jnp.float32),
                pltpu.VMEM((count, blocks_x * size_y, size_z), jnp.float32),
                pltpu.SemaphoreType.DMA((len(pieces),)),
            ],
        ),
        out_shape=jax.ShapeDtypeStruct((count, blocks_x, blocks_y, blocks_z), jnp.float32),
    )(offsets, *[piece[0] for piece in pieces], pool_z)


def conv_apply(padded, conv_weight, conv_bias):
    channels, span_x, span_y, span_z = padded.shape
    size_x, size_y, size_z = (span_x - 2, span_y - 2, span_z - 2)
    patches = jnp.stack(
        [
            padded[:, step_x : step_x + size_x, step_y : step_y + size_y, step_z : step_z + size_z]
            for step_x in range(3)
            for step_y in range(3)
            for step_z in range(3)
        ],
        axis=1,
    )
    patches = patches.reshape(channels * 27, size_x * size_y * size_z)
    matrix = conv_weight.reshape(conv_weight.shape[0], channels * 27)
    result = jnp.dot(
        matrix, patches, precision=lax.Precision.HIGHEST, preferred_element_type=jnp.float32
    )
    result = result + conv_bias[:, None]
    return result.reshape(conv_weight.shape[0], size_x, size_y * size_z)


def group_sum_windows(coarse, axis):
    count = lax.axis_size(axis)
    rows = coarse.shape[2] // count
    rimmed = jnp.pad(coarse, ((0, 0), (0, 0), (1, 1), (0, 0)))
    windows = jnp.stack(
        [lax.slice_in_dim(rimmed, k, k + (count - 1) * rows + 1, stride=rows, axis=2) for k in range(rows + 2)]
    )
    windows = jnp.moveaxis(windows, 3, 0)
    shape = windows.shape[1:]
    received = lax.all_to_all(windows.reshape(count, -1), axis, 0, 0, tiled=True)
    return jnp.moveaxis(received.sum(axis=0).reshape(shape), 0, 2)


def local(
    source_prev,
    source_now,
    receiver_prev,
    receiver_now,
    courant,
    source_cells,
    wavelet,
    receiver_cells,
    receiver_data,
    offsets,
    conv_weight,
    conv_bias,
):
    cells_x, size_y, size_z = courant.shape
    slab_index = lax.axis_index("gx")
    first_x = slab_index * cells_x
    previous = jnp.stack([source_prev[0], receiver_prev[0]])
    current = jnp.stack([source_now[0], receiver_now[0]])
    current_wide, previous_wide, courant_wide = input_halo(current, previous, courant, "gx")
    source_fields = inject(cells_x + 2, first_x - 1, source_cells[0], wavelet[0], size_y, size_z)
    receiver_fields = inject(cells_x + 2, first_x - 1, receiver_cells[0], receiver_data[0], size_y, size_z)
    levels = []
    for step_index in range(2):
        sources = jnp.stack([source_fields[step_index], receiver_fields[step_index]])
        if step_index == 0:
            step_previous, step_extended, step_courant = previous_wide, current_wide, courant_wide
        else:
            sources = sources[:, 1:-1]
            step_previous, step_extended, step_courant = current, levels[0], courant
        advanced = laplace_step(step_previous, step_extended, step_courant, sources)
        levels.append(advanced)
    levels_full = list(levels)
    levels[0] = levels[0][:, 1:-1]
    fields = jnp.concatenate(levels, axis=0)
    width = HMAX + 4
    low, high = halo_pieces(fields, "gx", width)
    pieces = [
        (low, 0, 0, 0, width),
        (levels_full[0], 0, width, 1, cells_x),
        (levels_full[1], 2, width, 0, cells_x),
        (high, 0, width + cells_x, 0, width),
    ]
    coarse = offset_image(pieces, offsets, HMAX, cells_x + 8)
    summed = group_sum_windows(coarse, "shot")
    window = jnp.pad(summed, ((0, 0), (0, 0), (0, 0), (1, 1)))
    return conv_apply(window, conv_weight, conv_bias)


def solution(mesh):
    in_specs = (
        P("shot", "gx", None, None),
        P("shot", "gx", None, None),
        P("shot", "gx", None, None),
        P("shot", "gx", None, None),
        P("gx", None, None),
        P("shot", None),
        P("shot", None, None),
        P("shot", None),
        P("shot", None, None),
        P(),
        P(),
        P(),
    )
    out_specs = P(None, "gx", "shot")
    return jax.shard_map(local, mesh=mesh, in_specs=in_specs, out_specs=out_specs, check_vma=False)
```

```python
import jax
import jax.numpy as jnp
from jax import lax
from jax.experimental import pallas as pl
from jax.experimental.pallas import tpu as pltpu
from jax.sharding import PartitionSpec as P

HMAX = 8


def padded_2(block, sides, width):
    for axis, dim in sides:
        count = lax.axis_size(axis)
        forward = [(i, i + 1) for i in range(count - 1)]
        backward = [(target, source) for source, target in forward]
        low = lax.ppermute(
            lax.slice_in_dim(block, block.shape[dim] - width, None, axis=dim), axis, forward
        )
        high = lax.ppermute(lax.slice_in_dim(block, 0, width, axis=dim), axis, backward)
        block = jnp.concatenate([low, block, high], axis=dim)
    return block


def halo_pieces(block, axis, width):
    count = lax.axis_size(axis)
    forward = [(i, i + 1) for i in range(count - 1)]
    backward = [(target, source) for source, target in forward]
    low = lax.ppermute(block[:, block.shape[1] - width :], axis, forward)
    high = lax.ppermute(block[:, :width], axis, backward)
    return low, high


def input_halo(current, previous, courant, axis):
    count = lax.axis_size(axis)
    forward = [(i, i + 1) for i in range(count - 1)]
    backward = [(target, source) for source, target in forward]
    fields, cells_x, size_y, size_z = current.shape

    def pack(now_planes, prev_planes, courant_planes):
        return jnp.concatenate(
            [now_planes.reshape(-1, size_y, size_z), prev_planes.reshape(-1, size_y, size_z), courant_planes]
        )

    def unpack(planes):
        now_planes = planes[: 2 * fields].reshape(fields, 2, size_y, size_z)
        prev_planes = planes[2 * fields : 3 * fields].reshape(fields, 1, size_y, size_z)
        return now_planes, prev_planes, planes[3 * fields :]

    low = lax.ppermute(
        pack(current[:, -2:], previous[:, -1:], courant[-1:]), axis, forward
    )
    high = lax.ppermute(pack(current[:, :2], previous[:, :1], courant[:1]), axis, backward)
    low_now, low_prev, low_courant = unpack(low)
    high_now, high_prev, high_courant = unpack(high)
    current_wide = jnp.concatenate([low_now, current, high_now], axis=1)
    previous_wide = jnp.concatenate([low_prev, previous, high_prev], axis=1)
    courant_wide = jnp.concatenate([low_courant, courant, high_courant], axis=0)
    return current_wide, previous_wide, courant_wide


def bf16_parts(value):
    high = value.astype(jnp.bfloat16)
    rest = value - high.astype(jnp.float32)
    middle = rest.astype(jnp.bfloat16)
    low = (rest - middle.astype(jnp.float32)).astype(jnp.bfloat16)
    return (high, middle, low)


def rounded_parts(value):
    high = lax.reduce_precision(value, exponent_bits=8, mantissa_bits=7)
    rest = value - high
    middle = lax.reduce_precision(rest, exponent_bits=8, mantissa_bits=7)
    low = rest - middle
    return (high.astype(jnp.bfloat16), middle.astype(jnp.bfloat16), low.astype(jnp.bfloat16))


def inject(cells_here, first_x, cell_index, amplitudes, size_y, size_z):
    plane_size = size_y * size_z
    column = cell_index // plane_size
    within = cell_index % plane_size
    row = (column - first_x) * size_y + within // size_z
    rows = (jnp.arange(cells_here * size_y)[:, None] == row[None, :]).astype(jnp.bfloat16)
    at_z = jnp.arange(size_z)[None, :] == (within % size_z)[:, None]
    fields = []
    for amplitude in amplitudes:
        placed = jnp.where(at_z, amplitude[:, None], 0.0)
        parts = jnp.concatenate(rounded_parts(placed), axis=1)
        sums = jnp.dot(rows, parts, preferred_element_type=jnp.float32)
        total = sums[:, :size_z] + sums[:, size_z : 2 * size_z] + sums[:, 2 * size_z :]
        fields.append(total.reshape(cells_here, size_y, size_z))
    return fields


def laplace_step(previous, extended, courant, sources):
    center = extended[:, 1:-1]
    padded = jnp.pad(center, ((0, 0), (0, 0), (1, 1), (1, 1)))
    laplace = extended[:, 2:] + extended[:, :-2]
    laplace = laplace + padded[:, :, 2:, 1:-1] + padded[:, :, :-2, 1:-1]
    laplace = laplace + padded[:, :, 1:-1, 2:] + padded[:, :, 1:-1, :-2] - 6.0 * center
    return 2.0 * center - previous + courant * laplace + sources


def pooling(size, group):
    fine = jnp.arange(size)[:, None] // group
    coarse = jnp.arange(size // group)[None, :]
    return (fine == coarse).astype(jnp.float32)


def split_dot(left, right, split_left):
    total = None
    if split_left:
        pieces = [(piece, right.astype(jnp.bfloat16)) for piece in bf16_parts(left)]
    else:
        pieces = [(left.astype(jnp.bfloat16), piece) for piece in bf16_parts(right)]
    for a, b in pieces:
        term = jnp.dot(a, b, preferred_element_type=jnp.float32)
        total = term if total is None else total + term
    return total


def offset_image(pieces, offsets, margin, cells_x):
    size_y, size_z = pieces[0][0].shape[2:]
    fields = max(first + array.shape[0] for array, first, _, _, _ in pieces)
    span_x = max(at + span for _, _, at, _, span in pieces)
    count = offsets.shape[0]
    blocks_x, blocks_y, blocks_z = cells_x // 4, size_y // 4, size_z // 4
    pool_z = pooling(size_z, 4)

    def kernel(offsets_ref, *refs):
        piece_refs = refs[: len(pieces)]
        pool_z_ref, out_ref, wide_ref, sum_ref, semaphores = refs[len(pieces) :]
        copies = []
        for k, (piece_ref, (array, first, at, taken, span)) in enumerate(zip(piece_refs, pieces)):
            source = piece_ref.at[:, taken : taken + span] if span != array.shape[1] else piece_ref
            target = wide_ref.at[first : first + array.shape[0], at : at + span]
            copies.append(pltpu.make_async_copy(source, target, semaphores.at[k]))
        for copy in copies:
            copy.start()
        high_at = max(at for _, _, at, _, _ in pieces)
        early = [block for block in range(blocks_x) if 4 * block + 3 + 2 * margin <= high_at - 1]
        late = [block for block in range(blocks_x) if block not in early]
        waited = [copy for copy, piece in zip(copies, pieces) if piece[2] < high_at]
        for copy in waited:
            copy.wait()

        def products(block_list):
            for index in range(count):
                offset_value = offsets_ref[index]
                forward = margin + offset_value
                backward = margin - offset_value
                for block in block_list:
                    total = None
                    for step in range(4):
                        x = block * 4 + step
                        term = (
                            wide_ref[0, forward + x] * wide_ref[1, backward + x]
                            + wide_ref[2, forward + x] * wide_ref[3, backward + x]
                        )
                        total = term if total is None else total + term
                    sum_ref[index, block * size_y : (block + 1) * size_y, :] = total

        products(early)
        for copy, piece in zip(copies, pieces):
            if piece[2] >= high_at:
                copy.wait()
        products(late)
        for index in range(count):
            pooled_y = None
            for step in range(4):
                rows = sum_ref.at[index][pl.ds(step, blocks_x * blocks_y, stride=4), :]
                pooled_y = rows if pooled_y is None else pooled_y + rows
            pooled = split_dot(pooled_y, pool_z_ref[...], True)
            out_ref[index, :, 1 : blocks_y + 1] = (pooled * (1.0 / 64.0)).reshape(blocks_x, blocks_y, blocks_z)
            out_ref[index, :, 0:1] = jnp.zeros((blocks_x, 1, blocks_z), jnp.float32)
            out_ref[index, :, blocks_y + 1 :] = jnp.zeros((blocks_x, 1, blocks_z), jnp.float32)

    return pl.pallas_call(
        kernel,
        grid_spec=pltpu.PrefetchScalarGridSpec(
            num_scalar_prefetch=1,
            grid=(1,),
            in_specs=[pl.BlockSpec(memory_space=pl.ANY) for _ in pieces]
            + [pl.BlockSpec((size_z, blocks_z), lambda i, offsets_ref: (0, 0))],
            out_specs=pl.BlockSpec((count, blocks_x, blocks_y + 2, blocks_z), lambda i, offsets_ref: (0, 0, 0, 0)),
            scratch_shapes=[
                pltpu.VMEM((fields, span_x, size_y, size_z), jnp.float32),
                pltpu.VMEM((count, blocks_x * size_y, size_z), jnp.float32),
                pltpu.SemaphoreType.DMA((len(pieces),)),
            ],
        ),
        out_shape=jax.ShapeDtypeStruct((count, blocks_x, blocks_y + 2, blocks_z), jnp.float32),
    )(offsets, *[piece[0] for piece in pieces], pool_z)


def conv_apply(padded, conv_weight, conv_bias):
    channels, span_x, span_y, span_z = padded.shape
    size_x, size_y, size_z = (span_x - 2, span_y - 2, span_z - 2)
    patches = jnp.stack(
        [
            padded[:, step_x : step_x + size_x, step_y : step_y + size_y, step_z : step_z + size_z]
            for step_x in range(3)
            for step_y in range(3)
            for step_z in range(3)
        ],
        axis=1,
    )
    patches = patches.reshape(channels * 27, size_x * size_y * size_z)
    matrix = conv_weight.reshape(conv_weight.shape[0], channels * 27)
    result = jnp.dot(
        matrix, patches, precision=lax.Precision.HIGHEST, preferred_element_type=jnp.float32
    )
    result = result + conv_bias[:, None]
    return result.reshape(conv_weight.shape[0], size_x, size_y * size_z)


def group_sum_windows(coarse, axis):
    count = lax.axis_size(axis)
    rimmed = coarse
    rows = (coarse.shape[2] - 2) // count
    windows = jnp.stack(
        [lax.slice_in_dim(rimmed, k, k + (count - 1) * rows + 1, stride=rows, axis=2) for k in range(rows + 2)]
    )
    windows = jnp.moveaxis(windows, 3, 0)
    shape = windows.shape[1:]
    received = lax.all_to_all(windows.reshape(count, -1), axis, 0, 0, tiled=True)
    return jnp.moveaxis(received.sum(axis=0).reshape(shape), 0, 2)


def local(
    source_prev,
    source_now,
    receiver_prev,
    receiver_now,
    courant,
    source_cells,
    wavelet,
    receiver_cells,
    receiver_data,
    offsets,
    conv_weight,
    conv_bias,
):
    cells_x, size_y, size_z = courant.shape
    slab_index = lax.axis_index("gx")
    first_x = slab_index * cells_x
    previous = jnp.stack([source_prev[0], receiver_prev[0]])
    current = jnp.stack([source_now[0], receiver_now[0]])
    current_wide, previous_wide, courant_wide = input_halo(current, previous, courant, "gx")
    source_fields = inject(cells_x + 2, first_x - 1, source_cells[0], wavelet[0], size_y, size_z)
    receiver_fields = inject(cells_x + 2, first_x - 1, receiver_cells[0], receiver_data[0], size_y, size_z)
    levels = []
    for step_index in range(2):
        sources = jnp.stack([source_fields[step_index], receiver_fields[step_index]])
        if step_index == 0:
            step_previous, step_extended, step_courant = previous_wide, current_wide, courant_wide
        else:
            sources = sources[:, 1:-1]
            step_previous, step_extended, step_courant = current, levels[0], courant
        advanced = laplace_step(step_previous, step_extended, step_courant, sources)
        levels.append(advanced)
    levels_full = list(levels)
    levels[0] = levels[0][:, 1:-1]
    fields = jnp.concatenate(levels, axis=0)
    width = HMAX + 4
    low, high = halo_pieces(fields, "gx", width)
    pieces = [
        (low, 0, 0, 0, width),
        (levels_full[0], 0, width, 1, cells_x),
        (levels_full[1], 2, width, 0, cells_x),
        (high, 0, width + cells_x, 0, width),
    ]
    coarse = offset_image(pieces, offsets, HMAX, cells_x + 8)
    summed = group_sum_windows(coarse, "shot")
    window = jnp.pad(summed, ((0, 0), (0, 0), (0, 0), (1, 1)))
    return conv_apply(window, conv_weight, conv_bias)


def solution(mesh):
    in_specs = (
        P("shot", "gx", None, None),
        P("shot", "gx", None, None),
        P("shot", "gx", None, None),
        P("shot", "gx", None, None),
        P("gx", None, None),
        P("shot", None),
        P("shot", None, None),
        P("shot", None),
        P("shot", None, None),
        P(),
        P(),
        P(),
    )
    out_specs = P(None, "gx", "shot")
    return jax.shard_map(local, mesh=mesh, in_specs=in_specs, out_specs=out_specs, check_vma=False)
```

```python
import jax
import jax.numpy as jnp
from jax import lax
from jax.experimental import pallas as pl
from jax.experimental.pallas import tpu as pltpu
from jax.sharding import PartitionSpec as P

HMAX = 8


def padded_2(block, sides, width):
    for axis, dim in sides:
        count = lax.axis_size(axis)
        forward = [(i, i + 1) for i in range(count - 1)]
        backward = [(target, source) for source, target in forward]
        low = lax.ppermute(
            lax.slice_in_dim(block, block.shape[dim] - width, None, axis=dim), axis, forward
        )
        high = lax.ppermute(lax.slice_in_dim(block, 0, width, axis=dim), axis, backward)
        block = jnp.concatenate([low, block, high], axis=dim)
    return block


def halo_pieces(block, axis, width):
    count = lax.axis_size(axis)
    forward = [(i, i + 1) for i in range(count - 1)]
    backward = [(target, source) for source, target in forward]
    low = lax.ppermute(block[:, block.shape[1] - width :], axis, forward)
    high = lax.ppermute(block[:, :width], axis, backward)
    return low, high


def input_halo(current, previous, courant, axis):
    count = lax.axis_size(axis)
    forward = [(i, i + 1) for i in range(count - 1)]
    backward = [(target, source) for source, target in forward]
    fields, cells_x, size_y, size_z = current.shape

    def pack(now_planes, prev_planes, courant_planes):
        return jnp.concatenate(
            [now_planes.reshape(-1, size_y, size_z), prev_planes.reshape(-1, size_y, size_z), courant_planes]
        )

    def unpack(planes):
        now_planes = planes[: 2 * fields].reshape(fields, 2, size_y, size_z)
        prev_planes = planes[2 * fields : 3 * fields].reshape(fields, 1, size_y, size_z)
        return now_planes, prev_planes, planes[3 * fields :]

    low = lax.ppermute(
        pack(current[:, -2:], previous[:, -1:], courant[-1:]), axis, forward
    )
    high = lax.ppermute(pack(current[:, :2], previous[:, :1], courant[:1]), axis, backward)
    low_now, low_prev, low_courant = unpack(low)
    high_now, high_prev, high_courant = unpack(high)
    current_wide = jnp.concatenate([low_now, current, high_now], axis=1)
    previous_wide = jnp.concatenate([low_prev, previous, high_prev], axis=1)
    courant_wide = jnp.concatenate([low_courant, courant, high_courant], axis=0)
    return current_wide, previous_wide, courant_wide


def bf16_parts(value):
    high = value.astype(jnp.bfloat16)
    rest = value - high.astype(jnp.float32)
    middle = rest.astype(jnp.bfloat16)
    low = (rest - middle.astype(jnp.float32)).astype(jnp.bfloat16)
    return (high, middle, low)


def rounded_parts(value):
    high = lax.reduce_precision(value, exponent_bits=8, mantissa_bits=7)
    rest = value - high
    middle = lax.reduce_precision(rest, exponent_bits=8, mantissa_bits=7)
    low = rest - middle
    return (high.astype(jnp.bfloat16), middle.astype(jnp.bfloat16), low.astype(jnp.bfloat16))


def inject(cells_here, first_x, cell_index, amplitudes, size_y, size_z):
    plane_size = size_y * size_z
    column = cell_index // plane_size
    within = cell_index % plane_size
    row = (column - first_x) * size_y + within // size_z
    rows = (jnp.arange(cells_here * size_y)[:, None] == row[None, :]).astype(jnp.bfloat16)
    at_z = jnp.arange(size_z)[None, :] == (within % size_z)[:, None]
    fields = []
    for amplitude in amplitudes:
        placed = jnp.where(at_z, amplitude[:, None], 0.0)
        parts = jnp.concatenate(rounded_parts(placed), axis=1)
        sums = jnp.dot(rows, parts, preferred_element_type=jnp.float32)
        total = sums[:, :size_z] + sums[:, size_z : 2 * size_z] + sums[:, 2 * size_z :]
        fields.append(total.reshape(cells_here, size_y, size_z))
    return fields


def laplace_step(previous, extended, courant, sources):
    center = extended[:, 1:-1]
    padded = jnp.pad(center, ((0, 0), (0, 0), (1, 1), (1, 1)))
    laplace = extended[:, 2:] + extended[:, :-2]
    laplace = laplace + padded[:, :, 2:, 1:-1] + padded[:, :, :-2, 1:-1]
    laplace = laplace + padded[:, :, 1:-1, 2:] + padded[:, :, 1:-1, :-2] - 6.0 * center
    return 2.0 * center - previous + courant * laplace + sources


def pooling(size, group):
    fine = jnp.arange(size)[:, None] // group
    coarse = jnp.arange(size // group)[None, :]
    return (fine == coarse).astype(jnp.float32)


def split_dot(left, right, split_left):
    total = None
    if split_left:
        pieces = [(piece, right.astype(jnp.bfloat16)) for piece in bf16_parts(left)]
    else:
        pieces = [(left.astype(jnp.bfloat16), piece) for piece in bf16_parts(right)]
    for a, b in pieces:
        term = jnp.dot(a, b, preferred_element_type=jnp.float32)
        total = term if total is None else total + term
    return total


def offset_image(pieces, offsets, margin, cells_x):
    size_y, size_z = pieces[0][0].shape[2:]
    fields = max(first + array.shape[0] for array, first, _, _, _ in pieces)
    span_x = max(at + span for _, _, at, _, span in pieces)
    count = offsets.shape[0]
    blocks_x, blocks_y, blocks_z = cells_x // 4, size_y // 4, size_z // 4
    pool_z = pooling(size_z, 4)

    def kernel(offsets_ref, *refs):
        piece_refs = refs[: len(pieces)]
        pool_z_ref, out_ref, wide_ref, sum_ref, semaphores = refs[len(pieces) :]
        copies = []
        for k, (piece_ref, (array, first, at, taken, span)) in enumerate(zip(piece_refs, pieces)):
            source = piece_ref.at[:, taken : taken + span] if span != array.shape[1] else piece_ref
            target = wide_ref.at[first : first + array.shape[0], at : at + span]
            copies.append(pltpu.make_async_copy(source, target, semaphores.at[k]))
        for copy in copies:
            copy.start()
        high_at = max(at for _, _, at, _, _ in pieces)
        early = [block for block in range(blocks_x) if 4 * block + 3 + 2 * margin <= high_at - 1]
        late = [block for block in range(blocks_x) if block not in early]
        waited = [copy for copy, piece in zip(copies, pieces) if piece[2] < high_at]
        for copy in waited:
            copy.wait()

        def products(block_list):
            for index in range(count):
                offset_value = offsets_ref[index]
                forward = margin + offset_value
                backward = margin - offset_value
                for block in block_list:
                    total = None
                    for step in range(4):
                        x = block * 4 + step
                        term = (
                            wide_ref[0, forward + x] * wide_ref[1, backward + x]
                            + wide_ref[2, forward + x] * wide_ref[3, backward + x]
                        )
                        total = term if total is None else total + term
                    sum_ref[index, block * size_y : (block + 1) * size_y, :] = total

        products(early)
        for copy, piece in zip(copies, pieces):
            if piece[2] >= high_at:
                copy.wait()
        products(late)
        for index in range(count):
            pooled_y = None
            for step in range(4):
                rows = sum_ref.at[index][pl.ds(step, blocks_x * blocks_y, stride=4), :]
                pooled_y = rows if pooled_y is None else pooled_y + rows
            high = pooled_y.astype(jnp.bfloat16)
            low = (pooled_y - high.astype(jnp.float32)).astype(jnp.bfloat16)
            pool_z_values = pool_z_ref[...].astype(jnp.bfloat16)
            pooled = jnp.dot(high, pool_z_values, preferred_element_type=jnp.float32) + jnp.dot(
                low, pool_z_values, preferred_element_type=jnp.float32
            )
            out_ref[index] = (pooled * (1.0 / 64.0)).reshape(blocks_x, blocks_y, blocks_z)

    return pl.pallas_call(
        kernel,
        grid_spec=pltpu.PrefetchScalarGridSpec(
            num_scalar_prefetch=1,
            grid=(1,),
            in_specs=[pl.BlockSpec(memory_space=pl.ANY) for _ in pieces]
            + [pl.BlockSpec((size_z, blocks_z), lambda i, offsets_ref: (0, 0))],
            out_specs=pl.BlockSpec((count, blocks_x, blocks_y, blocks_z), lambda i, offsets_ref: (0, 0, 0, 0)),
            scratch_shapes=[
                pltpu.VMEM((fields, span_x, size_y, size_z), jnp.float32),
                pltpu.VMEM((count, blocks_x * size_y, size_z), jnp.float32),
                pltpu.SemaphoreType.DMA((len(pieces),)),
            ],
        ),
        out_shape=jax.ShapeDtypeStruct((count, blocks_x, blocks_y, blocks_z), jnp.float32),
    )(offsets, *[piece[0] for piece in pieces], pool_z)


def conv_apply(padded, conv_weight, conv_bias):
    channels, span_x, span_y, span_z = padded.shape
    size_x, size_y, size_z = (span_x - 2, span_y - 2, span_z - 2)
    patches = jnp.stack(
        [
            padded[:, step_x : step_x + size_x, step_y : step_y + size_y, step_z : step_z + size_z]
            for step_x in range(3)
            for step_y in range(3)
            for step_z in range(3)
        ],
        axis=1,
    )
    patches = patches.reshape(channels * 27, size_x * size_y * size_z)
    matrix = conv_weight.reshape(conv_weight.shape[0], channels * 27)
    result = jnp.dot(
        matrix, patches, precision=lax.Precision.HIGHEST, preferred_element_type=jnp.float32
    )
    result = result + conv_bias[:, None]
    return result.reshape(conv_weight.shape[0], size_x, size_y * size_z)


def group_sum_windows(coarse, axis):
    count = lax.axis_size(axis)
    rows = coarse.shape[2] // count
    rimmed = jnp.pad(coarse, ((0, 0), (0, 0), (1, 1), (0, 0)))
    windows = jnp.stack(
        [lax.slice_in_dim(rimmed, k, k + (count - 1) * rows + 1, stride=rows, axis=2) for k in range(rows + 2)]
    )
    windows = jnp.moveaxis(windows, 3, 0)
    shape = windows.shape[1:]
    received = lax.all_to_all(windows.reshape(count, -1), axis, 0, 0, tiled=True)
    return jnp.moveaxis(received.sum(axis=0).reshape(shape), 0, 2)


def local(
    source_prev,
    source_now,
    receiver_prev,
    receiver_now,
    courant,
    source_cells,
    wavelet,
    receiver_cells,
    receiver_data,
    offsets,
    conv_weight,
    conv_bias,
):
    cells_x, size_y, size_z = courant.shape
    slab_index = lax.axis_index("gx")
    first_x = slab_index * cells_x
    previous = jnp.stack([source_prev[0], receiver_prev[0]])
    current = jnp.stack([source_now[0], receiver_now[0]])
    current_wide, previous_wide, courant_wide = input_halo(current, previous, courant, "gx")
    source_fields = inject(cells_x + 2, first_x - 1, source_cells[0], wavelet[0], size_y, size_z)
    receiver_fields = inject(cells_x + 2, first_x - 1, receiver_cells[0], receiver_data[0], size_y, size_z)
    levels = []
    for step_index in range(2):
        sources = jnp.stack([source_fields[step_index], receiver_fields[step_index]])
        if step_index == 0:
            step_previous, step_extended, step_courant = previous_wide, current_wide, courant_wide
        else:
            sources = sources[:, 1:-1]
            step_previous, step_extended, step_courant = current, levels[0], courant
        advanced = laplace_step(step_previous, step_extended, step_courant, sources)
        levels.append(advanced)
    levels_full = list(levels)
    levels[0] = levels[0][:, 1:-1]
    fields = jnp.concatenate(levels, axis=0)
    width = HMAX + 4
    low, high = halo_pieces(fields, "gx", width)
    pieces = [
        (low, 0, 0, 0, width),
        (levels_full[0], 0, width, 1, cells_x),
        (levels_full[1], 2, width, 0, cells_x),
        (high, 0, width + cells_x, 0, width),
    ]
    coarse = offset_image(pieces, offsets, HMAX, cells_x + 8)
    summed = group_sum_windows(coarse, "shot")
    window = jnp.pad(summed, ((0, 0), (0, 0), (0, 0), (1, 1)))
    return conv_apply(window, conv_weight, conv_bias)


def solution(mesh):
    in_specs = (
        P("shot", "gx", None, None),
        P("shot", "gx", None, None),
        P("shot", "gx", None, None),
        P("shot", "gx", None, None),
        P("gx", None, None),
        P("shot", None),
        P("shot", None, None),
        P("shot", None),
        P("shot", None, None),
        P(),
        P(),
        P(),
    )
    out_specs = P(None, "gx", "shot")
    return jax.shard_map(local, mesh=mesh, in_specs=in_specs, out_specs=out_specs, check_vma=False)
```
